128 devices in a mesh: seq: 32 (over y, z, core), tp: 4 (over x).
Axes of the slice: x: 4, y: 4, z: 4, core: 2. Of those that a mesh axis runs over, the one named last changes fastest.
Arguments:
- rollout_rows: bfloat16 [16384, 8192], P('seq', 'tp'), may hold values from -100 to 100
- plan: int32 [16384], P('seq'), may hold values from 0 to 16383, as said below
- segment_ids: int32 [16384], P('seq'), may hold values from 0 to 256, as said below
- norm_gain: float32 [8192], replicated, may hold values from 0.1 to 1.9
- q_weight: bfloat16 [8192, 4096], P('seq', 'tp'), may hold values from -0.0625 to 0.0625
- k_weight: bfloat16 [8192, 512], P('seq', 'tp'), may hold values from -0.0625 to 0.0625
- v_weight: bfloat16 [8192, 512], P('seq', 'tp'), may hold values from -0.0625 to 0.0625
- q_bias: float32 [4096], P('tp'), may hold values from -40 to 40
- k_bias: float32 [512], P('tp'), may hold values from -40 to 40
- v_bias: float32 [512], P('tp'), may hold values from -3 to 3
Outputs:
- context: bfloat16 [16384, 4096], P('seq', 'tp')
The draws below stay inside these ranges and needn't reach their ends.
Inputs may be any that keep to these rules, and one draw needn't show every extreme that they name: plan is a permutation of the learner rows; rollout row r goes to learner shard plan[r] // 512. The rows of one device go 16 to every learner shard, except 20 rows to one shard and 12 rows to another. `segment_ids`: within each learner shard the ids start at 0, never fall and rise by one at each new sequence; each sequence has 1 to 256 rows and one sequence of every shard has exactly 256; no sequence crosses a shard.
All inputs are finite; a program needn't handle non-finite values.
Results may differ from the reference program's by a relative error of at most 0.012.
The reference program's roundings to bfloat16 on the way count: a program that leaves them out, or rounds other values in their place, can miss the bound.
Values may be sent and summed in bfloat16 or wider, within the bound.
No kernel may reach another device: no remote copies, remote signals or barrier semaphores. Data moves between devices by JAX's collectives and lax.ppermute only.
A program may use at most 128 MiB of HBM per device.

```python
import math
import jax
import jax.numpy as jnp
from jax import lax

D = 8192
HEAD = 128
QHEADS = 32
KVHEADS = 4
TOK_DEV = 512
SEQ_MAX = 256
TOKENS = 16384


def draw_rollout_rows(key, part):
    row_key, col_key, main_key = jax.random.split(key, 3)
    row_scale = jnp.exp(jax.random.uniform(row_key, (TOKENS, 1), jnp.float32, math.log(0.3), math.log(3.0)))
    col_scale = jnp.exp(jax.random.uniform(col_key, (1, D), jnp.float32, math.log(0.3), math.log(3.0)))
    result = jax.random.normal(main_key, (TOKENS, D), jnp.float32) * row_scale * col_scale
    return result.astype(jnp.bfloat16)


def draw_q_bias(key, part):
    return 0.5 * jax.random.normal(jax.random.fold_in(key, 204), (QHEADS * HEAD,), jnp.float32)


def draw_k_bias(key, part):
    return 0.5 * jax.random.normal(jax.random.fold_in(key, 304), (KVHEADS * HEAD,), jnp.float32)


def shuffled(subkey):
    return jax.random.permutation(subkey, TOK_DEV)


def draw_plan(key, part):
    shard_count = TOKENS // TOK_DEV
    share_rows = TOK_DEV // shard_count
    extra_rows = share_rows // 4
    sigma_key, source_key, dest_key = jax.random.split(key, 3)
    sigma = jax.random.permutation(sigma_key, shard_count).astype(jnp.int32)
    shifted = jnp.roll(sigma, -1)
    columns = jnp.arange(shard_count, dtype=jnp.int32)
    counts = share_rows + extra_rows * (columns[None, :] == sigma[:, None]).astype(jnp.int32) - extra_rows * (columns[None, :] == shifted[:, None]).astype(jnp.int32)
    inclusive = jnp.cumsum(counts, axis=1)
    exclusive = inclusive - counts
    items = jnp.arange(TOK_DEV, dtype=jnp.int32)
    labels = jnp.sum((inclusive[:, None, :] <= items[None, :, None]).astype(jnp.int32), axis=2)
    ranks = items[None, :] - jnp.take_along_axis(exclusive, labels, axis=1)
    column_start = jnp.cumsum(counts, axis=0) - counts
    within = jnp.take_along_axis(column_start, labels, axis=1) + ranks
    dest_perm = jax.vmap(shuffled)(jax.random.split(dest_key, shard_count)).astype(jnp.int32)
    landing = dest_perm[labels, within]
    targets = labels * TOK_DEV + landing
    source_perm = jax.vmap(shuffled)(jax.random.split(source_key, shard_count)).astype(jnp.int32)
    result = jnp.zeros((shard_count, TOK_DEV), jnp.int32).at[jnp.arange(shard_count)[:, None], source_perm].set(targets)
    return result.reshape(TOKENS).astype(jnp.int32)


def draw_segment_ids(key, part):
    shard_count = TOKENS // TOK_DEV
    length_key, pick_key, shard_key = jax.random.split(key, 3)
    lengths = jax.random.randint(length_key, (shard_count, TOK_DEV), 1, SEQ_MAX + 1)
    chosen = jax.random.randint(pick_key, (shard_count, 1), 0, 2)
    special = jax.random.randint(shard_key, (), 0, shard_count)
    slot_index = jnp.arange(TOK_DEV)[None, :]
    is_special = jnp.arange(shard_count)[:, None] == special
    lengths = jnp.where(is_special, 1, lengths)
    lengths = jnp.where(slot_index == chosen, SEQ_MAX, lengths)
    ends = jnp.minimum(jnp.cumsum(lengths, axis=1), TOK_DEV)
    marks = jnp.zeros((shard_count, TOK_DEV + 1), jnp.int32).at[jnp.arange(shard_count)[:, None], ends].set(1)
    result = jnp.cumsum(marks[:, :TOK_DEV], axis=1)
    return result.reshape(TOKENS).astype(jnp.int32)


def steps_of(stream_key, extent, shards, least, high):
    level, own = 1.0, jax.random.fold_in(stream_key, 6)
    for position, blocks in shards:
        draws = jnp.exp(jax.random.uniform(jax.random.fold_in(own, position), (blocks,), jnp.float32, least / len(shards), high / len(shards)))
        level = level * jnp.repeat(draws, extent[position] // blocks).reshape([-1 if axis == position else 1 for axis in range(len(extent))])
    return level


def bell_draw(rng, dims, deviation, bound, shards=(), kind=jnp.bfloat16):
    values = deviation * jax.random.normal(rng, dims, jnp.float32)
    if shards:
        values = values * steps_of(rng, dims, shards, -0.22, 0.18)
    return jnp.clip(values, -bound, bound).astype(kind)


def setup_inputs(seed: int = 0) -> dict:
    streams_of = jax.random.split(jax.random.key(seed), 11)
    rollout_rows = draw_rollout_rows(jax.random.fold_in(streams_of[10], 71), 0)
    plan = draw_plan(jax.random.fold_in(streams_of[10], 71), 0)
    segment_ids = draw_segment_ids(jax.random.fold_in(streams_of[10], 71), 0)
    norm_gain = jnp.clip(1.0 + 0.18 * jax.random.normal(streams_of[3], (D,), jnp.float32), 0.1, 1.9)
    q_weight = bell_draw(streams_of[4], (D, QHEADS * HEAD), D ** -0.5, 0.0625, ((0, 32), (1, 4)))
    k_weight = bell_draw(streams_of[5], (D, KVHEADS * HEAD), D ** -0.5, 0.0625, ((0, 32), (1, 4)))
    v_weight = bell_draw(streams_of[6], (D, KVHEADS * HEAD), D ** -0.5, 0.0625, ((0, 32), (1, 4)))
    q_bias = draw_q_bias(jax.random.fold_in(streams_of[10], 71), 0)
    k_bias = draw_k_bias(jax.random.fold_in(streams_of[10], 71), 0)
    v_bias = bell_draw(streams_of[9], (KVHEADS * HEAD,), 0.5, 3.0, ((0, 4),), jnp.float32)
    return dict(rollout_rows=rollout_rows, plan=plan, segment_ids=segment_ids, norm_gain=norm_gain, q_weight=q_weight, k_weight=k_weight, v_weight=v_weight, q_bias=q_bias, k_bias=k_bias, v_bias=v_bias)


EPS = 1e-06
ROPE_BASE = 1000000.0

def rotate(tensor, positions):
    half_size = tensor.shape[-1] // 2
    frequency = jnp.exp(jnp.arange(half_size, dtype=jnp.float32) * (-2.0 * math.log(ROPE_BASE) / tensor.shape[-1]))
    angles = positions.astype(jnp.float32)[:, None] * frequency[None, :]
    cosine = jnp.cos(angles)[:, None, :]
    sine_part = jnp.sin(angles)[:, None, :]
    front_half = tensor[..., :half_size]
    back_half = tensor[..., half_size:]
    return jnp.concatenate([front_half * cosine - back_half * sine_part, back_half * cosine + front_half * sine_part], axis=-1)

def positions_of(segments):
    length = segments.shape[-1]
    counter = jnp.broadcast_to(jnp.arange(length, dtype=jnp.int32), segments.shape)
    starts = jnp.concatenate([jnp.ones(segments.shape[:-1] + (1,), dtype=bool), segments[..., 1:] != segments[..., :-1]], axis=-1)
    marked = jnp.where(starts, counter, jnp.zeros_like(counter))
    leading = lax.cummax(marked, axis=segments.ndim - 1)
    return counter - leading

def reference(rollout_rows, plan, segment_ids, norm_gain, q_weight, k_weight, v_weight, q_bias, k_bias, v_bias):
    shard_count = TOKENS // TOK_DEV
    learner = jnp.zeros_like(rollout_rows).at[plan].set(rollout_rows)
    widened = learner.astype(jnp.float32)
    mean_sq = lax.optimization_barrier(jnp.mean(widened * widened, axis=-1, keepdims=True))
    normed = (widened * lax.rsqrt(mean_sq + EPS) * norm_gain).astype(jnp.bfloat16)
    queries = jnp.dot(normed, q_weight, preferred_element_type=jnp.float32) + q_bias
    key_proj = jnp.dot(normed, k_weight, preferred_element_type=jnp.float32) + k_bias
    value_proj = (jnp.dot(normed, v_weight, preferred_element_type=jnp.float32) + v_bias).astype(jnp.bfloat16)
    shard_segments = segment_ids.reshape(shard_count, TOK_DEV)
    positions = positions_of(shard_segments).reshape(TOKENS)
    q_rot = rotate(queries.reshape(TOKENS, QHEADS, HEAD), positions).astype(jnp.bfloat16)
    k_rot = rotate(key_proj.reshape(TOKENS, KVHEADS, HEAD), positions).astype(jnp.bfloat16)
    value_heads = value_proj.reshape(TOKENS, KVHEADS, HEAD)
    group_size = QHEADS // KVHEADS
    counter = jnp.arange(TOK_DEV, dtype=jnp.int32)

    def one_shard(items):
        q_shard, k_shard, v_shard, seg_shard = items
        q_float = q_shard.astype(jnp.float32).reshape(TOK_DEV, KVHEADS, group_size, HEAD)
        scores = jnp.einsum('qkgd,pkd->kgqp', q_float, k_shard.astype(jnp.float32)) / math.sqrt(HEAD)
        allowed = (seg_shard[:, None] == seg_shard[None, :]) & (counter[:, None] >= counter[None, :])
        scores = jnp.where(allowed[None, None], scores, -jnp.inf)
        highest = lax.optimization_barrier(jnp.max(scores, axis=-1, keepdims=True))
        expo = jnp.exp(scores - highest)
        probs = (expo / lax.optimization_barrier(jnp.sum(expo, axis=-1, keepdims=True))).astype(jnp.bfloat16)
        mixed = jnp.einsum('kgqp,pkd->qkgd', probs.astype(jnp.float32), v_shard.astype(jnp.float32))
        return mixed.astype(jnp.bfloat16).reshape(TOK_DEV, QHEADS * HEAD)
    contexts = lax.map(one_shard, (q_rot.reshape(shard_count, TOK_DEV, QHEADS, HEAD), k_rot.reshape(shard_count, TOK_DEV, KVHEADS, HEAD), value_heads.reshape(shard_count, TOK_DEV, KVHEADS, HEAD), shard_segments))
    return contexts.reshape(TOKENS, QHEADS * HEAD)
```

```python
import math

import jax
import jax.numpy as jnp
from jax import lax
from jax.sharding import Mesh
from jax.sharding import PartitionSpec as P


HEAD = 128


EPS = 1e-06
ROPE_BASE = 1000000.0

CHIPS = "chips"
CORE = "core"
SEQ = (CHIPS, CORE)
TP = "tp"


def rotate(tensor, positions):
    half_size = tensor.shape[-1] // 2
    frequency = jnp.exp(
        jnp.arange(half_size, dtype=jnp.float32) * (-2.0 * math.log(ROPE_BASE) / tensor.shape[-1])
    )
    angles = positions.astype(jnp.float32)[:, None] * frequency[None, :]
    cosine = jnp.cos(angles)[:, None, :]
    sine_part = jnp.sin(angles)[:, None, :]
    front_half = tensor[..., :half_size]
    back_half = tensor[..., half_size:]
    return jnp.concatenate(
        [front_half * cosine - back_half * sine_part, back_half * cosine + front_half * sine_part],
        axis=-1,
    )


def positions_of(segments):
    length = segments.shape[-1]
    counter = jnp.arange(length, dtype=jnp.int32)
    starts = jnp.concatenate([jnp.ones((1,), dtype=bool), segments[1:] != segments[:-1]])
    marked = jnp.where(starts, counter, jnp.zeros_like(counter))
    return counter - lax.cummax(marked, axis=0)


def make_local(chip_count, core_count, tp_count):
    peer_count = chip_count * core_count

    def body(
        rollout_rows, plan, segment_ids, norm_gain, q_weight, k_weight, v_weight, q_bias, k_bias, v_bias
    ):
        row_count, width = rollout_rows.shape
        slots_each = row_count // peer_count + row_count // (4 * peer_count)
        slot_total = peer_count * slots_each
        q_cols = q_weight.shape[1]
        k_cols = k_weight.shape[1]
        depth = q_weight.shape[0]

        weights = jnp.concatenate([q_weight, k_weight, v_weight], axis=1)
        chip_weights = lax.all_gather(weights, CHIPS, axis=0, tiled=False)
        full_weights = lax.all_gather(chip_weights, CORE, axis=0, tiled=False)

        target = plan // row_count
        learner_slot = plan % row_count
        matches = (target[:, None] == jnp.arange(peer_count, dtype=jnp.int32)[None, :]).astype(
            jnp.int32
        )
        ranking = jnp.sum((jnp.cumsum(matches, axis=0) - 1) * matches, axis=1)
        flat_slot = target * slots_each + ranking
        slot_numbers = jnp.arange(slot_total, dtype=jnp.int32)
        row_numbers = jnp.arange(row_count, dtype=jnp.int32)
        slot_hits = flat_slot[None, :] == slot_numbers[:, None]
        parcels = (
            jnp.sum(jnp.where(slot_hits, learner_slot[None, :] + 1, 0), axis=1) - 1
        ).reshape(peer_count, slots_each)
        labels = lax.all_to_all(parcels, SEQ, split_axis=0, concat_axis=0, tiled=True)
        picked = jnp.dot(
            slot_hits.astype(jnp.bfloat16), rollout_rows, preferred_element_type=jnp.float32
        ).astype(jnp.bfloat16)
        arrived = lax.all_to_all(
            picked.reshape(peer_count, slots_each, width),
            SEQ,
            split_axis=0,
            concat_axis=0,
            tiled=True,
        )
        label_hits = labels.reshape(slot_total)[None, :] == row_numbers[:, None]
        learner_part = jnp.dot(
            label_hits.astype(jnp.bfloat16),
            arrived.reshape(slot_total, width),
            preferred_element_type=jnp.float32,
        ).astype(jnp.bfloat16)
        spread = jnp.broadcast_to(learner_part[None], (tp_count, row_count, width))
        quarters = lax.all_to_all(spread, TP, split_axis=0, concat_axis=0, tiled=True)
        widened = quarters.astype(jnp.float32)
        mean_sq = jnp.sum(widened * widened, axis=(0, 2), keepdims=True) / (width * tp_count)
        gain = norm_gain.reshape(tp_count, 1, width)
        normed = (widened * lax.rsqrt(mean_sq + EPS) * gain).astype(jnp.bfloat16)
        normed = normed.transpose(1, 0, 2).reshape(row_count, chip_count, core_count, depth)
        projected = jnp.einsum(
            "rhcj,chjn->rn", normed, full_weights, preferred_element_type=jnp.float32
        )
        queries = projected[:, :q_cols]
        key_proj = projected[:, q_cols : q_cols + k_cols]
        value_proj = projected[:, q_cols + k_cols :]
        local_heads = q_cols // HEAD
        local_groups = k_cols // HEAD
        group_size = local_heads // local_groups
        positions = positions_of(segment_ids)
        q_rot = rotate((queries + q_bias).reshape(row_count, local_heads, HEAD), positions).astype(
            jnp.bfloat16
        )
        q_rot = q_rot.reshape(row_count, local_groups, group_size, HEAD)
        k_rot = rotate((key_proj + k_bias).reshape(row_count, local_groups, HEAD), positions).astype(
            jnp.bfloat16
        )
        value_heads = (value_proj + v_bias).astype(jnp.bfloat16).reshape(row_count, local_groups, HEAD)
        block_rows = min(512, row_count)
        row_index = jnp.arange(row_count, dtype=jnp.int32)
        scores = jnp.einsum(
            "qkgd,pkd->kgqp", q_rot, k_rot, preferred_element_type=jnp.float32
        ) / math.sqrt(HEAD)
        allowed = (segment_ids[0:block_rows, None] == segment_ids[None, :block_rows]) & (
            row_index[0:block_rows, None] >= row_index[None, :block_rows]
        )
        scores = jnp.where(allowed[None, None], scores, -jnp.inf)
        highest = jnp.max(scores, axis=-1, keepdims=True)
        expo = jnp.exp(scores - highest)
        probs = (expo / jnp.sum(expo, axis=-1, keepdims=True)).astype(jnp.bfloat16)
        mixed = jnp.einsum("kgqp,pkd->qkgd", probs, value_heads, preferred_element_type=jnp.float32)
        outputs = mixed.astype(jnp.bfloat16).reshape(block_rows, local_heads * HEAD)
        return outputs

    return body


def solution(mesh):
    seq_count, tp_count = mesh.devices.shape
    core_count = 2
    chip_count = seq_count // core_count
    split = Mesh(mesh.devices.reshape(chip_count, core_count, tp_count), (CHIPS, CORE, TP))
    in_specs = (
        P(SEQ, TP),
        P(SEQ),
        P(SEQ),
        P(),
        P(SEQ, TP),
        P(SEQ, TP),
        P(SEQ, TP),
        P(TP),
        P(TP),
        P(TP),
    )
    out_specs = P(SEQ, TP)
    return jax.shard_map(
        make_local(chip_count, core_count, tp_count),
        mesh=split,
        in_specs=in_specs,
        out_specs=out_specs,
        check_vma=False,
    )
```

```python
import math

import jax
import jax.numpy as jnp
from jax import lax
from jax.sharding import Mesh
from jax.sharding import PartitionSpec as P


HEAD = 128


EPS = 1e-06
ROPE_BASE = 1000000.0

CHIPS = "chips"
CORE = "core"
SEQ = (CHIPS, CORE)
TP = "tp"


def rotate(tensor, positions):
    half_size = tensor.shape[-1] // 2
    frequency = jnp.exp(
        jnp.arange(half_size, dtype=jnp.float32) * (-2.0 * math.log(ROPE_BASE) / tensor.shape[-1])
    )
    angles = positions.astype(jnp.float32)[:, None] * frequency[None, :]
    cosine = jnp.cos(angles)[:, None, :]
    sine_part = jnp.sin(angles)[:, None, :]
    front_half = tensor[..., :half_size]
    back_half = tensor[..., half_size:]
    return jnp.concatenate(
        [front_half * cosine - back_half * sine_part, back_half * cosine + front_half * sine_part],
        axis=-1,
    )


def positions_of(segments):
    length = segments.shape[-1]
    counter = jnp.arange(length, dtype=jnp.int32)
    starts = jnp.concatenate([jnp.ones((1,), dtype=bool), segments[1:] != segments[:-1]])
    marked = jnp.where(starts, counter, jnp.zeros_like(counter))
    return counter - lax.cummax(marked, axis=0)


def make_local(chip_count, core_count, tp_count):
    peer_count = chip_count * core_count

    def body(
        rollout_rows, plan, segment_ids, norm_gain, q_weight, k_weight, v_weight, q_bias, k_bias, v_bias
    ):
        row_count, width = rollout_rows.shape
        slots_each = row_count // peer_count + row_count // (4 * peer_count)
        q_cols = q_weight.shape[1]
        k_cols = k_weight.shape[1]
        depth = q_weight.shape[0]

        weights = jnp.concatenate([q_weight, k_weight, v_weight], axis=1)
        own_weights = lax.all_gather(weights, CHIPS, axis=0, tiled=False)
        other_weights = lax.ppermute(
            own_weights, CORE, [(c, (c + 1) % core_count) for c in range(core_count)]
        )

        target = plan // row_count
        learner_slot = plan % row_count
        matches = (target[:, None] == jnp.arange(peer_count, dtype=jnp.int32)[None, :]).astype(
            jnp.int32
        )
        ranking = jnp.sum((jnp.cumsum(matches, axis=0) - 1) * matches, axis=1)
        slot_hits = (target[None, None, :] == jnp.arange(peer_count, dtype=jnp.int32)[:, None, None]) & (
            ranking[None, None, :] == jnp.arange(slots_each, dtype=jnp.int32)[None, :, None]
        )
        parcels = jnp.sum(jnp.where(slot_hits, learner_slot[None, None, :] + 1, 0), axis=2) - 1
        labels = lax.all_to_all(parcels, SEQ, split_axis=0, concat_axis=0, tiled=True)
        picked = jnp.einsum(
            "psr,rf->psf",
            slot_hits.astype(jnp.bfloat16),
            rollout_rows,
            preferred_element_type=jnp.float32,
        ).astype(jnp.bfloat16)
        arrived = lax.all_to_all(picked, SEQ, split_axis=0, concat_axis=0, tiled=True)
        row_numbers = jnp.arange(row_count, dtype=jnp.int32)
        label_hits = labels[None, :, :] == row_numbers[:, None, None]
        learner_part = jnp.einsum(
            "rps,psf->rf",
            label_hits.astype(jnp.bfloat16),
            arrived,
            preferred_element_type=jnp.float32,
        ).astype(jnp.bfloat16)

        to_right = [(t, (t + 1) % tp_count) for t in range(tp_count)]
        to_left = [(t, (t - 1) % tp_count) for t in range(tp_count)]
        half = width // 2
        from_left = lax.ppermute(learner_part, TP, to_right)
        from_right = lax.ppermute(learner_part, TP, to_left)
        far_a = lax.ppermute(from_left[:, :half], TP, to_right)
        far_b = lax.ppermute(from_right[:, half:], TP, to_left)
        far = jnp.concatenate([far_a, far_b], axis=1)
        tp_index = lax.axis_index(TP)
        by_offset = jnp.stack([learner_part, from_left, far, from_right])
        order = (tp_index - jnp.arange(tp_count, dtype=jnp.int32)) % tp_count
        inverse = jnp.argsort(order)
        quarters = jnp.take(by_offset, inverse, axis=0)
        widened = quarters.astype(jnp.float32)
        mean_sq = jnp.sum(widened * widened, axis=(0, 2), keepdims=True) / (width * tp_count)
        gain = norm_gain.reshape(tp_count, 1, width)
        normed = (widened * lax.rsqrt(mean_sq + EPS) * gain).astype(jnp.bfloat16)
        normed = normed.transpose(1, 0, 2).reshape(row_count, chip_count, core_count, depth)
        core_index = lax.axis_index(CORE)
        own_cols = jnp.take(normed, core_index, axis=2)
        other_cols = jnp.take(normed, (core_index + 1) % core_count, axis=2)
        projected = jnp.einsum(
            "rhj,hjn->rn", own_cols, own_weights, preferred_element_type=jnp.float32
        ) + jnp.einsum("rhj,hjn->rn", other_cols, other_weights, preferred_element_type=jnp.float32)
        queries = projected[:, :q_cols]
        key_proj = projected[:, q_cols : q_cols + k_cols]
        value_proj = projected[:, q_cols + k_cols :]
        local_heads = q_cols // HEAD
        local_groups = k_cols // HEAD
        group_size = local_heads // local_groups
        positions = positions_of(segment_ids)
        q_rot = rotate((queries + q_bias).reshape(row_count, local_heads, HEAD), positions).astype(
            jnp.bfloat16
        )
        q_rot = q_rot.reshape(row_count, local_groups, group_size, HEAD)
        k_rot = rotate((key_proj + k_bias).reshape(row_count, local_groups, HEAD), positions).astype(
            jnp.bfloat16
        )
        value_heads = (value_proj + v_bias).astype(jnp.bfloat16).reshape(row_count, local_groups, HEAD)
        block_rows = min(512, row_count)
        row_index = jnp.arange(row_count, dtype=jnp.int32)
        scores = jnp.einsum(
            "qkgd,pkd->kgqp", q_rot, k_rot, preferred_element_type=jnp.float32
        ) / math.sqrt(HEAD)
        allowed = (segment_ids[0:block_rows, None] == segment_ids[None, :block_rows]) & (
            row_index[0:block_rows, None] >= row_index[None, :block_rows]
        )
        scores = jnp.where(allowed[None, None], scores, -jnp.inf)
        highest = jnp.max(scores, axis=-1, keepdims=True)
        expo = jnp.exp(scores - highest)
        probs = (expo / jnp.sum(expo, axis=-1, keepdims=True)).astype(jnp.bfloat16)
        mixed = jnp.einsum("kgqp,pkd->qkgd", probs, value_heads, preferred_element_type=jnp.float32)
        outputs = mixed.astype(jnp.bfloat16).reshape(block_rows, local_heads * HEAD)
        return outputs

    return body


def solution(mesh):
    seq_count, tp_count = mesh.devices.shape
    core_count = 2
    chip_count = seq_count // core_count
    split = Mesh(mesh.devices.reshape(chip_count, core_count, tp_count), (CHIPS, CORE, TP))
    in_specs = (
        P(SEQ, TP),
        P(SEQ),
        P(SEQ),
        P(),
        P(SEQ, TP),
        P(SEQ, TP),
        P(SEQ, TP),
        P(TP),
        P(TP),
        P(TP),
    )
    out_specs = P(SEQ, TP)
    return jax.shard_map(
        make_local(chip_count, core_count, tp_count),
        mesh=split,
        in_specs=in_specs,
        out_specs=out_specs,
        check_vma=False,
    )
```

```python
import math

import jax
import jax.numpy as jnp
from jax import lax
from jax.sharding import Mesh
from jax.sharding import PartitionSpec as P


HEAD = 128


EPS = 1e-06
ROPE_BASE = 1000000.0

CHIPS = "chips"
CORE = "core"
SEQ = (CHIPS, CORE)
TP = "tp"


def rotate(tensor, positions):
    half_size = tensor.shape[-1] // 2
    frequency = jnp.exp(
        jnp.arange(half_size, dtype=jnp.float32) * (-2.0 * math.log(ROPE_BASE) / tensor.shape[-1])
    )
    angles = positions.astype(jnp.float32)[:, None] * frequency[None, :]
    cosine = jnp.cos(angles)[:, None, :]
    sine_part = jnp.sin(angles)[:, None, :]
    front_half = tensor[..., :half_size]
    back_half = tensor[..., half_size:]
    return jnp.concatenate(
        [front_half * cosine - back_half * sine_part, back_half * cosine + front_half * sine_part],
        axis=-1,
    )


def positions_of(segments):
    length = segments.shape[-1]
    counter = jnp.arange(length, dtype=jnp.int32)
    starts = jnp.concatenate([jnp.ones((1,), dtype=bool), segments[1:] != segments[:-1]])
    marked = jnp.where(starts, counter, jnp.zeros_like(counter))
    return counter - lax.cummax(marked, axis=0)


def make_local(chip_count, core_count, tp_count):
    peer_count = chip_count * core_count

    def body(
        rollout_rows, plan, segment_ids, norm_gain, q_weight, k_weight, v_weight, q_bias, k_bias, v_bias
    ):
        row_count, width = rollout_rows.shape
        slots_each = row_count // peer_count + row_count // (4 * peer_count)
        q_cols = q_weight.shape[1]
        k_cols = k_weight.shape[1]
        depth = q_weight.shape[0]

        weights = jnp.concatenate([q_weight, k_weight, v_weight], axis=1)
        own_weights = lax.all_gather(weights, CHIPS, axis=0, tiled=False)
        other_weights = lax.ppermute(
            own_weights, CORE, [(c, (c + 1) % core_count) for c in range(core_count)]
        )

        target = plan // row_count
        learner_slot = plan % row_count
        matches = (target[:, None] == jnp.arange(peer_count, dtype=jnp.int32)[None, :]).astype(
            jnp.int32
        )
        ranking = jnp.sum((jnp.cumsum(matches, axis=0) - 1) * matches, axis=1)
        slot_hits = (target[None, None, :] == jnp.arange(peer_count, dtype=jnp.int32)[:, None, None]) & (
            ranking[None, None, :] == jnp.arange(slots_each, dtype=jnp.int32)[None, :, None]
        )
        tagged = jnp.sum(jnp.where(slot_hits, learner_slot[None, None, :] + 1, 0), axis=2)
        tag_row = jnp.concatenate(
            [
                (tagged // 32).astype(jnp.bfloat16),
                (tagged % 32).astype(jnp.bfloat16),
                jnp.zeros((peer_count, width - 2 * slots_each), jnp.bfloat16),
            ],
            axis=1,
        )
        picked = jnp.einsum(
            "psr,rf->psf",
            slot_hits.astype(jnp.bfloat16),
            rollout_rows,
            preferred_element_type=jnp.float32,
        ).astype(jnp.bfloat16)
        payload = jnp.concatenate([picked, tag_row[:, None, :]], axis=1)
        arrived = lax.all_to_all(payload, SEQ, split_axis=0, concat_axis=0, tiled=True)
        tags = arrived[:, slots_each, : 2 * slots_each].astype(jnp.int32)
        labels = tags[:, :slots_each] * 32 + tags[:, slots_each:] - 1
        row_numbers = jnp.arange(row_count, dtype=jnp.int32)
        label_hits = labels[None, :, :] == row_numbers[:, None, None]
        learner_part = jnp.einsum(
            "rps,psf->rf",
            label_hits.astype(jnp.bfloat16),
            arrived[:, :slots_each, :],
            preferred_element_type=jnp.float32,
        ).astype(jnp.bfloat16)

        to_right = [(t, (t + 1) % tp_count) for t in range(tp_count)]
        to_left = [(t, (t - 1) % tp_count) for t in range(tp_count)]
        half = width // 2
        from_left = lax.ppermute(learner_part, TP, to_right)
        from_right = lax.ppermute(learner_part, TP, to_left)
        far_a = lax.ppermute(from_left[:, :half], TP, to_right)
        far_b = lax.ppermute(from_right[:, half:], TP, to_left)
        far = jnp.concatenate([far_a, far_b], axis=1)
        pieces = [learner_part, from_left, far, from_right]
        tp_index = lax.axis_index(TP)
        wide = [p.astype(jnp.float32) for p in pieces]
        total_sq = sum(jnp.sum(w * w, axis=-1, keepdims=True) for w in wide)
        scale = lax.rsqrt(total_sq / (width * tp_count) + EPS)
        normed = []
        for k, w in enumerate(wide):
            quarter = (tp_index - k) % tp_count
            gain = lax.dynamic_slice_in_dim(norm_gain, quarter * width, width)
            normed.append((w * scale * gain).astype(jnp.bfloat16))

        core_index = lax.axis_index(CORE)
        natural = jnp.where(
          core_index == 0,
          jnp.stack([own_weights, other_weights], axis=1),
          jnp.stack([other_weights, own_weights], axis=1),
        ).reshape(chip_count * core_count * depth, own_weights.shape[-1])
        projected = None
        for k, piece in enumerate(normed):
            quarter = (tp_index - k) % tp_count
            rows = lax.dynamic_slice_in_dim(natural, quarter * width, width, axis=0)
            part = jnp.dot(piece, rows, preferred_element_type=jnp.float32)
            projected = part if projected is None else projected + part
        queries = projected[:, :q_cols]
        key_proj = projected[:, q_cols : q_cols + k_cols]
        value_proj = projected[:, q_cols + k_cols :]
        local_heads = q_cols // HEAD
        local_groups = k_cols // HEAD
        group_size = local_heads // local_groups
        positions = positions_of(segment_ids)
        q_rot = rotate((queries + q_bias).reshape(row_count, local_heads, HEAD), positions).astype(
            jnp.bfloat16
        )
        q_rot = q_rot.reshape(row_count, local_groups, group_size, HEAD)
        k_rot = rotate((key_proj + k_bias).reshape(row_count, local_groups, HEAD), positions).astype(
            jnp.bfloat16
        )
        value_heads = (value_proj + v_bias).astype(jnp.bfloat16).reshape(row_count, local_groups, HEAD)
        block_rows = min(512, row_count)
        row_index = jnp.arange(row_count, dtype=jnp.int32)
        scores = jnp.einsum(
            "qkgd,pkd->kgqp", q_rot, k_rot, preferred_element_type=jnp.float32
        ) / math.sqrt(HEAD)
        allowed = (segment_ids[0:block_rows, None] == segment_ids[None, :block_rows]) & (
            row_index[0:block_rows, None] >= row_index[None, :block_rows]
        )
        scores = jnp.where(allowed[None, None], scores, -jnp.inf)
        highest = jnp.max(scores, axis=-1, keepdims=True)
        expo = jnp.exp(scores - highest)
        probs = (expo / jnp.sum(expo, axis=-1, keepdims=True)).astype(jnp.bfloat16)
        mixed = jnp.einsum("kgqp,pkd->qkgd", probs, value_heads, preferred_element_type=jnp.float32)
        outputs = mixed.astype(jnp.bfloat16).reshape(block_rows, local_heads * HEAD)
        return outputs

    return body


def solution(mesh):
    seq_count, tp_count = mesh.devices.shape
    core_count = 2
    chip_count = seq_count // core_count
    split = Mesh(mesh.devices.reshape(chip_count, core_count, tp_count), (CHIPS, CORE, TP))
    in_specs = (
        P(SEQ, TP),
        P(SEQ),
        P(SEQ),
        P(),
        P(SEQ, TP),
        P(SEQ, TP),
        P(SEQ, TP),
        P(TP),
        P(TP),
        P(TP),
    )
    out_specs = P(SEQ, TP)
    return jax.shard_map(
        make_local(chip_count, core_count, tp_count),
        mesh=split,
        in_specs=in_specs,
        out_specs=out_specs,
        check_vma=False,
    )
```

```python
import math

import jax
import jax.numpy as jnp
from jax import lax
from jax.sharding import Mesh
from jax.sharding import PartitionSpec as P


HEAD = 128


EPS = 1e-06
ROPE_BASE = 1000000.0

CHIPS = "chips"
CORE = "core"
SEQ = (CHIPS, CORE)
TP = "tp"


def rotate(tensor, positions):
    half_size = tensor.shape[-1] // 2
    frequency = jnp.exp(
        jnp.arange(half_size, dtype=jnp.float32) * (-2.0 * math.log(ROPE_BASE) / tensor.shape[-1])
    )
    angles = positions.astype(jnp.float32)[:, None] * frequency[None, :]
    cosine = jnp.cos(angles)[:, None, :]
    sine_part = jnp.sin(angles)[:, None, :]
    front_half = tensor[..., :half_size]
    back_half = tensor[..., half_size:]
    return jnp.concatenate(
        [front_half * cosine - back_half * sine_part, back_half * cosine + front_half * sine_part],
        axis=-1,
    )


def positions_of(segments):
    length = segments.shape[-1]
    counter = jnp.arange(length, dtype=jnp.int32)
    starts = jnp.concatenate([jnp.ones((1,), dtype=bool), segments[1:] != segments[:-1]])
    marked = jnp.where(starts, counter, jnp.zeros_like(counter))
    return counter - lax.cummax(marked, axis=0)


def make_local(chip_count, core_count, tp_count):
    peer_count = chip_count * core_count

    def body(
        rollout_rows, plan, segment_ids, norm_gain, q_weight, k_weight, v_weight, q_bias, k_bias, v_bias
    ):
        row_count, width = rollout_rows.shape
        slots_each = row_count // peer_count + row_count // (4 * peer_count)
        q_cols = q_weight.shape[1]
        k_cols = k_weight.shape[1]

        weights = jnp.concatenate([q_weight, k_weight, v_weight], axis=1)
        own_weights = lax.all_gather(weights, CHIPS, axis=0, tiled=False)
        other_weights = lax.ppermute(
            own_weights, CORE, [(c, (c + 1) % core_count) for c in range(core_count)]
        )

        target = plan // row_count
        learner_slot = plan % row_count
        matches = (target[:, None] == jnp.arange(peer_count, dtype=jnp.int32)[None, :]).astype(
            jnp.int32
        )
        ranking = jnp.sum((jnp.cumsum(matches, axis=0) - 1) * matches, axis=1)
        slot_hits = (target[None, None, :] == jnp.arange(peer_count, dtype=jnp.int32)[:, None, None]) & (
            ranking[None, None, :] == jnp.arange(slots_each, dtype=jnp.int32)[None, :, None]
        )
        tagged = jnp.sum(jnp.where(slot_hits, learner_slot[None, None, :] + 1, 0), axis=2)
        block = width // (4 * core_count)
        chunk = width // core_count
        tag_row = jnp.concatenate(
            [
                (tagged // 32).astype(jnp.bfloat16),
                (tagged % 32).astype(jnp.bfloat16),
                jnp.zeros((peer_count, chunk - 2 * slots_each), jnp.bfloat16),
            ],
            axis=1,
        )
        picked = jnp.einsum(
            "psr,rf->psf",
            slot_hits.astype(jnp.bfloat16),
            rollout_rows,
            preferred_element_type=jnp.float32,
        ).astype(jnp.bfloat16)
        split_cols = picked.reshape(chip_count, core_count, slots_each, 4, core_count, block)
        chunk_a = jnp.stack(
            [split_cols[:, c, :, :, c, :] for c in range(core_count)], axis=1
        ).reshape(peer_count, slots_each, chunk)
        chunk_b = jnp.stack(
            [split_cols[:, c, :, :, (c + 1) % core_count, :] for c in range(core_count)], axis=1
        ).reshape(peer_count, slots_each, chunk)
        payload_a = jnp.concatenate([chunk_a, tag_row[:, None, :]], axis=1)
        arrived_a = lax.all_to_all(payload_a, SEQ, split_axis=0, concat_axis=0, tiled=True)
        tags = arrived_a[:, slots_each, : 2 * slots_each].astype(jnp.int32)
        labels = tags[:, :slots_each] * 32 + tags[:, slots_each:] - 1
        row_numbers = jnp.arange(row_count, dtype=jnp.int32)
        label_hits = (labels[None, :, :] == row_numbers[:, None, None]).astype(jnp.bfloat16)

        def place(arrived):
            return jnp.einsum(
                "rps,psf->rf",
                label_hits,
                arrived[:, :slots_each, :],
                preferred_element_type=jnp.float32,
            ).astype(jnp.bfloat16)

        to_right = [(t, (t + 1) % tp_count) for t in range(tp_count)]
        to_left = [(t, (t - 1) % tp_count) for t in range(tp_count)]

        def ring(part):
            half = part.shape[1] // 2
            from_left = lax.ppermute(part, TP, to_right)
            from_right = lax.ppermute(part, TP, to_left)
            far_a = lax.ppermute(from_left[:, :half], TP, to_right)
            far_b = lax.ppermute(from_right[:, half:], TP, to_left)
            far = jnp.concatenate([far_a, far_b], axis=1)
            return [part, from_left, far, from_right]

        part_a = place(arrived_a)
        pieces_a = ring(part_a)
        arrived_b = lax.all_to_all(chunk_b, SEQ, split_axis=0, concat_axis=0, tiled=True)
        part_b = place(arrived_b)
        pieces_b = ring(part_b)

        wa = part_a.astype(jnp.float32)
        wb = part_b.astype(jnp.float32)
        own_sq = jnp.sum(wa * wa, axis=1) + jnp.sum(wb * wb, axis=1)
        others = [
            lax.ppermute(own_sq, TP, [(t, (t + k) % tp_count) for t in range(tp_count)])
            for k in range(1, tp_count)
        ]
        total_sq = own_sq
        for other in others:
            total_sq = total_sq + other
        scale = lax.rsqrt(total_sq / (width * tp_count) + EPS)[:, None]

        tp_index = lax.axis_index(TP)
        core_index = lax.axis_index(CORE)
        gain_blocks = norm_gain.reshape(tp_count, 4, core_count, block)
        projected = None
        for pieces, weights_of, core_of in (
            (pieces_a, own_weights, core_index),
            (pieces_b, other_weights, (core_index + 1) % core_count),
        ):
            for k, piece in enumerate(pieces):
                quarter = (tp_index - k) % tp_count
                gain = lax.dynamic_slice(
                    gain_blocks, (quarter, 0, core_of, 0), (1, 4, 1, block)
                ).reshape(chunk)
                normed = (piece.astype(jnp.float32) * scale * gain).astype(jnp.bfloat16)
                rows = lax.dynamic_slice_in_dim(weights_of, quarter * 4, 4, axis=0).reshape(
                    chunk, weights_of.shape[-1]
                )
                part = jnp.dot(normed, rows, preferred_element_type=jnp.float32)
                projected = part if projected is None else projected + part
        queries = projected[:, :q_cols]
        key_proj = projected[:, q_cols : q_cols + k_cols]
        value_proj = projected[:, q_cols + k_cols :]
        local_heads = q_cols // HEAD
        local_groups = k_cols // HEAD
        group_size = local_heads // local_groups
        positions = positions_of(segment_ids)
        q_rot = rotate((queries + q_bias).reshape(row_count, local_heads, HEAD), positions).astype(
            jnp.bfloat16
        )
        q_rot = q_rot.reshape(row_count, local_groups, group_size, HEAD)
        k_rot = rotate((key_proj + k_bias).reshape(row_count, local_groups, HEAD), positions).astype(
            jnp.bfloat16
        )
        value_heads = (value_proj + v_bias).astype(jnp.bfloat16).reshape(row_count, local_groups, HEAD)
        block_rows = min(512, row_count)
        row_index = jnp.arange(row_count, dtype=jnp.int32)
        scores = jnp.einsum(
            "qkgd,pkd->kgqp", q_rot, k_rot, preferred_element_type=jnp.float32
        ) / math.sqrt(HEAD)
        allowed = (segment_ids[0:block_rows, None] == segment_ids[None, :block_rows]) & (
            row_index[0:block_rows, None] >= row_index[None, :block_rows]
        )
        scores = jnp.where(allowed[None, None], scores, -jnp.inf)
        highest = jnp.max(scores, axis=-1, keepdims=True)
        expo = jnp.exp(scores - highest)
        probs = (expo / jnp.sum(expo, axis=-1, keepdims=True)).astype(jnp.bfloat16)
        mixed = jnp.einsum("kgqp,pkd->qkgd", probs, value_heads, preferred_element_type=jnp.float32)
        outputs = mixed.astype(jnp.bfloat16).reshape(block_rows, local_heads * HEAD)
        return outputs

    return body


def solution(mesh):
    seq_count, tp_count = mesh.devices.shape
    core_count = 2
    chip_count = seq_count // core_count
    split = Mesh(mesh.devices.reshape(chip_count, core_count, tp_count), (CHIPS, CORE, TP))
    in_specs = (
        P(SEQ, TP),
        P(SEQ),
        P(SEQ),
        P(),
        P(SEQ, TP),
        P(SEQ, TP),
        P(SEQ, TP),
        P(TP),
        P(TP),
        P(TP),
    )
    out_specs = P(SEQ, TP)
    return jax.shard_map(
        make_local(chip_count, core_count, tp_count),
        mesh=split,
        in_specs=in_specs,
        out_specs=out_specs,
        check_vma=False,
    )
```

```python
import math

import jax
import jax.numpy as jnp
from jax import lax
from jax.sharding import Mesh
from jax.sharding import PartitionSpec as P


HEAD = 128


EPS = 1e-06
ROPE_BASE = 1000000.0

CHIPS = "chips"
CORE = "core"
SEQ = (CHIPS, CORE)
TP = "tp"


def rotate(tensor, positions):
    half_size = tensor.shape[-1] // 2
    frequency = jnp.exp(
        jnp.arange(half_size, dtype=jnp.float32) * (-2.0 * math.log(ROPE_BASE) / tensor.shape[-1])
    )
    angles = positions.astype(jnp.float32)[:, None] * frequency[None, :]
    cosine = jnp.cos(angles)[:, None, :]
    sine_part = jnp.sin(angles)[:, None, :]
    front_half = tensor[..., :half_size]
    back_half = tensor[..., half_size:]
    return jnp.concatenate(
        [front_half * cosine - back_half * sine_part, back_half * cosine + front_half * sine_part],
        axis=-1,
    )


def positions_of(segments):
    length = segments.shape[-1]
    counter = jnp.arange(length, dtype=jnp.int32)
    starts = jnp.concatenate([jnp.ones((1,), dtype=bool), segments[1:] != segments[:-1]])
    marked = jnp.where(starts, counter, jnp.zeros_like(counter))
    return counter - lax.cummax(marked, axis=0)


def make_local(chip_count, core_count, tp_count):
    peer_count = chip_count * core_count

    def body(
        rollout_rows, plan, segment_ids, norm_gain, q_weight, k_weight, v_weight, q_bias, k_bias, v_bias
    ):
        row_count, width = rollout_rows.shape
        slots_each = row_count // peer_count + row_count // (4 * peer_count)
        q_cols = q_weight.shape[1]
        k_cols = k_weight.shape[1]


        weights = jnp.concatenate([q_weight, k_weight, v_weight], axis=1)
        own_weights = lax.all_gather(weights, CHIPS, axis=0, tiled=False)
        other_weights = lax.ppermute(
            own_weights, CORE, [(c, (c + 1) % core_count) for c in range(core_count)]
        )

        target = plan // row_count
        learner_slot = plan % row_count
        matches = (target[:, None] == jnp.arange(peer_count, dtype=jnp.int32)[None, :]).astype(
            jnp.int32
        )
        ranking = jnp.sum((jnp.cumsum(matches, axis=0) - 1) * matches, axis=1)
        slot_hits = (target[None, None, :] == jnp.arange(peer_count, dtype=jnp.int32)[:, None, None]) & (
            ranking[None, None, :] == jnp.arange(slots_each, dtype=jnp.int32)[None, :, None]
        )
        tagged = jnp.sum(jnp.where(slot_hits, learner_slot[None, None, :] + 1, 0), axis=2)
        tag_row = jnp.concatenate(
            [
                (tagged // 32).astype(jnp.bfloat16),
                (tagged % 32).astype(jnp.bfloat16),
                jnp.zeros((peer_count, width - 2 * slots_each), jnp.bfloat16),
            ],
            axis=1,
        )
        picked = jnp.einsum(
            "psr,rf->psf",
            slot_hits.astype(jnp.bfloat16),
            rollout_rows,
            preferred_element_type=jnp.float32,
        ).astype(jnp.bfloat16)
        payload = jnp.concatenate([picked, tag_row[:, None, :]], axis=1)
        arrived = lax.all_to_all(payload, SEQ, split_axis=0, concat_axis=0, tiled=True)
        tags = arrived[:, slots_each, : 2 * slots_each].astype(jnp.int32)
        labels = tags[:, :slots_each] * 32 + tags[:, slots_each:] - 1
        row_numbers = jnp.arange(row_count, dtype=jnp.int32)
        label_hits = labels[None, :, :] == row_numbers[:, None, None]
        learner_part = jnp.einsum(
            "rps,psf->rf",
            label_hits.astype(jnp.bfloat16),
            arrived[:, :slots_each, :],
            preferred_element_type=jnp.float32,
        ).astype(jnp.bfloat16)

        tp_index = lax.axis_index(TP)
        core_index = lax.axis_index(CORE)
        wide = learner_part.astype(jnp.float32)
        own_sq = jnp.sum(wide * wide, axis=-1)
        others = [
            lax.ppermute(own_sq, TP, [(t, (t + k) % tp_count) for t in range(tp_count)])
            for k in range(1, tp_count)
        ]
        total_sq = own_sq
        for other in others:
            total_sq = total_sq + other
        scale = lax.rsqrt(total_sq / (width * tp_count) + EPS)[:, None]

        to_right = [(t, (t + 1) % tp_count) for t in range(tp_count)]
        to_left = [(t, (t - 1) % tp_count) for t in range(tp_count)]
        half = width // 2
        from_left = lax.ppermute(learner_part, TP, to_right)
        from_right = lax.ppermute(learner_part, TP, to_left)
        far_a = lax.ppermute(from_left[:, :half], TP, to_right)
        far_b = lax.ppermute(from_right[:, half:], TP, to_left)
        far = jnp.concatenate([far_a, far_b], axis=1)
        pieces = [learner_part, from_left, far, from_right]

        block = width // (4 * core_count)
        span = 4 * block
        own_rows = own_weights.reshape(tp_count, span, own_weights.shape[-1])
        other_rows = other_weights.reshape(tp_count, span, own_weights.shape[-1])

        def core_block(x, c):
            return jnp.concatenate(
                [x[:, (hl * core_count + c) * block : (hl * core_count + c + 1) * block] for hl in range(4)],
                axis=1,
            )

        projected = None
        for k in (0, 1, 3, 2):
            piece = pieces[k]
            quarter = (tp_index - k) % tp_count
            gain = lax.dynamic_slice_in_dim(norm_gain, quarter * width, width)
            normed = (piece.astype(jnp.float32) * scale * gain).astype(jnp.bfloat16)
            first = core_block(normed, 0)
            second = core_block(normed, 1)
            mine = jnp.where(core_index == 0, first, second)
            theirs = jnp.where(core_index == 0, second, first)
            for cols, rows_of in ((mine, own_rows), (theirs, other_rows)):
                rows = lax.dynamic_index_in_dim(rows_of, quarter, axis=0, keepdims=False)
                part = jnp.dot(cols, rows, preferred_element_type=jnp.float32)
                projected = part if projected is None else projected + part
        queries = projected[:, :q_cols]
        key_proj = projected[:, q_cols : q_cols + k_cols]
        value_proj = projected[:, q_cols + k_cols :]
        local_heads = q_cols // HEAD
        local_groups = k_cols // HEAD
        group_size = local_heads // local_groups
        positions = positions_of(segment_ids)
        q_rot = rotate((queries + q_bias).reshape(row_count, local_heads, HEAD), positions).astype(
            jnp.bfloat16
        )
        q_rot = q_rot.reshape(row_count, local_groups, group_size, HEAD)
        k_rot = rotate((key_proj + k_bias).reshape(row_count, local_groups, HEAD), positions).astype(
            jnp.bfloat16
        )
        value_heads = (value_proj + v_bias).astype(jnp.bfloat16).reshape(row_count, local_groups, HEAD)
        block_rows = min(512, row_count)
        row_index = jnp.arange(row_count, dtype=jnp.int32)
        scores = jnp.einsum(
            "qkgd,pkd->kgqp", q_rot, k_rot, preferred_element_type=jnp.float32
        ) / math.sqrt(HEAD)
        allowed = (segment_ids[0:block_rows, None] == segment_ids[None, :block_rows]) & (
            row_index[0:block_rows, None] >= row_index[None, :block_rows]
        )
        scores = jnp.where(allowed[None, None], scores, -jnp.inf)
        highest = jnp.max(scores, axis=-1, keepdims=True)
        expo = jnp.exp(scores - highest)
        probs = (expo / jnp.sum(expo, axis=-1, keepdims=True)).astype(jnp.bfloat16)
        mixed = jnp.einsum("kgqp,pkd->qkgd", probs, value_heads, preferred_element_type=jnp.float32)
        outputs = mixed.astype(jnp.bfloat16).reshape(block_rows, local_heads * HEAD)
        return outputs

    return body


def solution(mesh):
    seq_count, tp_count = mesh.devices.shape
    core_count = 2
    chip_count = seq_count // core_count
    split = Mesh(mesh.devices.reshape(chip_count, core_count, tp_count), (CHIPS, CORE, TP))
    in_specs = (
        P(SEQ, TP),
        P(SEQ),
        P(SEQ),
        P(),
        P(SEQ, TP),
        P(SEQ, TP),
        P(SEQ, TP),
        P(TP),
        P(TP),
        P(TP),
    )
    out_specs = P(SEQ, TP)
    return jax.shard_map(
        make_local(chip_count, core_count, tp_count),
        mesh=split,
        in_specs=in_specs,
        out_specs=out_specs,
        check_vma=False,
    )
```

```python
import math

import jax
import jax.numpy as jnp
from jax import lax
from jax.sharding import Mesh
from jax.sharding import PartitionSpec as P


HEAD = 128


EPS = 1e-06
ROPE_BASE = 1000000.0

CHIPS = "chips"
CORE = "core"
SEQ = (CHIPS, CORE)
TP = "tp"


def rotate(tensor, positions):
    half_size = tensor.shape[-1] // 2
    frequency = jnp.exp(
        jnp.arange(half_size, dtype=jnp.float32) * (-2.0 * math.log(ROPE_BASE) / tensor.shape[-1])
    )
    angles = positions.astype(jnp.float32)[:, None] * frequency[None, :]
    cosine = jnp.cos(angles)[:, None, :]
    sine_part = jnp.sin(angles)[:, None, :]
    front_half = tensor[..., :half_size]
    back_half = tensor[..., half_size:]
    return jnp.concatenate(
        [front_half * cosine - back_half * sine_part, back_half * cosine + front_half * sine_part],
        axis=-1,
    )


def positions_of(segments):
    length = segments.shape[-1]
    counter = jnp.arange(length, dtype=jnp.int32)
    starts = jnp.concatenate([jnp.ones((1,), dtype=bool), segments[1:] != segments[:-1]])
    marked = jnp.where(starts, counter, jnp.zeros_like(counter))
    return counter - lax.cummax(marked, axis=0)


def make_local(chip_count, core_count, tp_count):
    peer_count = chip_count * core_count

    def body(
        rollout_rows, plan, segment_ids, norm_gain, q_weight, k_weight, v_weight, q_bias, k_bias, v_bias
    ):
        row_count, width = rollout_rows.shape
        slots_each = row_count // peer_count + row_count // (4 * peer_count)
        q_cols = q_weight.shape[1]
        k_cols = k_weight.shape[1]


        weights = jnp.concatenate([q_weight, k_weight, v_weight], axis=1)
        own_weights = lax.all_gather(weights, CHIPS, axis=0, tiled=False)
        other_weights = lax.ppermute(
            own_weights, CORE, [(c, (c + 1) % core_count) for c in range(core_count)]
        )

        target = plan // row_count
        learner_slot = plan % row_count
        matches = (target[:, None] == jnp.arange(peer_count, dtype=jnp.int32)[None, :]).astype(
            jnp.int32
        )
        ranking = jnp.sum((jnp.cumsum(matches, axis=0) - 1) * matches, axis=1)
        slot_hits = (target[None, None, :] == jnp.arange(peer_count, dtype=jnp.int32)[:, None, None]) & (
            ranking[None, None, :] == jnp.arange(slots_each, dtype=jnp.int32)[None, :, None]
        )
        tagged = jnp.sum(jnp.where(slot_hits, learner_slot[None, None, :] + 1, 0), axis=2)
        tag_row = jnp.concatenate(
            [
                (tagged // 32).astype(jnp.bfloat16),
                (tagged % 32).astype(jnp.bfloat16),
                jnp.zeros((peer_count, width - 2 * slots_each), jnp.bfloat16),
            ],
            axis=1,
        )
        picked = jnp.einsum(
            "psr,rf->psf",
            slot_hits.astype(jnp.bfloat16),
            rollout_rows,
            preferred_element_type=jnp.float32,
        ).astype(jnp.bfloat16)
        payload = jnp.concatenate([picked, tag_row[:, None, :]], axis=1)
        by_chip = payload.reshape(chip_count, core_count, slots_each + 1, width)
        crossed = lax.all_to_all(by_chip, CHIPS, split_axis=0, concat_axis=0, tiled=True)
        arrived = lax.all_to_all(
            crossed.transpose(1, 0, 2, 3), CORE, split_axis=0, concat_axis=0, tiled=True
        )
        tags = arrived[:, :, slots_each, : 2 * slots_each].astype(jnp.int32)
        labels = tags[:, :, :slots_each] * 32 + tags[:, :, slots_each:] - 1
        row_numbers = jnp.arange(row_count, dtype=jnp.int32)
        label_hits = labels[None] == row_numbers[:, None, None, None]
        learner_part = jnp.einsum(
            "rchs,chsf->rf",
            label_hits.astype(jnp.bfloat16),
            arrived[:, :, :slots_each, :],
            preferred_element_type=jnp.float32,
        ).astype(jnp.bfloat16)

        tp_index = lax.axis_index(TP)
        core_index = lax.axis_index(CORE)
        wide = learner_part.astype(jnp.float32)
        own_sq = jnp.sum(wide * wide, axis=-1)
        others = [
            lax.ppermute(own_sq, TP, [(t, (t + k) % tp_count) for t in range(tp_count)])
            for k in range(1, tp_count)
        ]
        total_sq = own_sq
        for other in others:
            total_sq = total_sq + other
        scale = lax.rsqrt(total_sq / (width * tp_count) + EPS)[:, None]

        to_right = [(t, (t + 1) % tp_count) for t in range(tp_count)]
        to_left = [(t, (t - 1) % tp_count) for t in range(tp_count)]
        half = width // 2
        from_left = lax.ppermute(learner_part, TP, to_right)
        from_right = lax.ppermute(learner_part, TP, to_left)
        far_a = lax.ppermute(from_left[:, :half], TP, to_right)
        far_b = lax.ppermute(from_right[:, half:], TP, to_left)
        far = jnp.concatenate([far_a, far_b], axis=1)
        pieces = [learner_part, from_left, far, from_right]

        block = width // (4 * core_count)
        span = 4 * block
        own_rows = own_weights.reshape(tp_count, span, own_weights.shape[-1])
        other_rows = other_weights.reshape(tp_count, span, own_weights.shape[-1])

        def core_block(x, c):
            return jnp.concatenate(
                [x[:, (hl * core_count + c) * block : (hl * core_count + c + 1) * block] for hl in range(4)],
                axis=1,
            )

        def normalize(piece, k, scale, norm_gain, tp_index):
            quarter = (tp_index - k) % tp_count
            gain = lax.dynamic_slice_in_dim(norm_gain, quarter * width, width)
            return (piece.astype(jnp.float32) * scale * gain).astype(jnp.bfloat16)

        def project(normed, k, tp_index, core_index):
            quarter = (tp_index - k) % tp_count
            first = core_block(normed, 0)
            second = core_block(normed, 1)
            mine = jnp.where(core_index == 0, first, second)
            theirs = jnp.where(core_index == 0, second, first)
            total = None
            for cols, rows_of in ((mine, own_rows), (theirs, other_rows)):
                rows = lax.dynamic_index_in_dim(rows_of, quarter, axis=0, keepdims=False)
                part = jnp.dot(cols, rows, preferred_element_type=jnp.float32)
                total = part if total is None else total + part
            return total

        projected = None
        for k in (0, 1, 3):
            normed = normalize(pieces[k], k, scale, norm_gain, tp_index)
            part = project(normed, k, tp_index, core_index)
            projected = part if projected is None else projected + part
        far_piece, far_scale, far_gain, far_tp, far_core = lax.optimization_barrier(
            (pieces[2], scale, norm_gain, tp_index, core_index)
        )
        normed = normalize(far_piece, 2, far_scale, far_gain, far_tp)
        projected = projected + project(normed, 2, far_tp, far_core)
        queries = projected[:, :q_cols]
        key_proj = projected[:, q_cols : q_cols + k_cols]
        value_proj = projected[:, q_cols + k_cols :]
        local_heads = q_cols // HEAD
        local_groups = k_cols // HEAD
        group_size = local_heads // local_groups
        positions = positions_of(segment_ids)
        q_rot = rotate((queries + q_bias).reshape(row_count, local_heads, HEAD), positions).astype(
            jnp.bfloat16
        )
        q_rot = q_rot.reshape(row_count, local_groups, group_size, HEAD)
        k_rot = rotate((key_proj + k_bias).reshape(row_count, local_groups, HEAD), positions).astype(
            jnp.bfloat16
        )
        value_heads = (value_proj + v_bias).astype(jnp.bfloat16).reshape(row_count, local_groups, HEAD)
        block_rows = min(512, row_count)
        row_index = jnp.arange(row_count, dtype=jnp.int32)
        scores = jnp.einsum(
            "qkgd,pkd->kgqp", q_rot, k_rot, preferred_element_type=jnp.float32
        ) / math.sqrt(HEAD)
        allowed = (segment_ids[0:block_rows, None] == segment_ids[None, :block_rows]) & (
            row_index[0:block_rows, None] >= row_index[None, :block_rows]
        )
        scores = jnp.where(allowed[None, None], scores, -jnp.inf)
        highest = jnp.max(scores, axis=-1, keepdims=True)
        expo = jnp.exp(scores - highest)
        probs = (expo / jnp.sum(expo, axis=-1, keepdims=True)).astype(jnp.bfloat16)
        mixed = jnp.einsum("kgqp,pkd->qkgd", probs, value_heads, preferred_element_type=jnp.float32)
        outputs = mixed.astype(jnp.bfloat16).reshape(block_rows, local_heads * HEAD)
        return outputs

    return body


def solution(mesh):
    seq_count, tp_count = mesh.devices.shape
    core_count = 2
    chip_count = seq_count // core_count
    split = Mesh(mesh.devices.reshape(chip_count, core_count, tp_count), (CHIPS, CORE, TP))
    in_specs = (
        P(SEQ, TP),
        P(SEQ),
        P(SEQ),
        P(),
        P(SEQ, TP),
        P(SEQ, TP),
        P(SEQ, TP),
        P(TP),
        P(TP),
        P(TP),
    )
    out_specs = P(SEQ, TP)
    return jax.shard_map(
        make_local(chip_count, core_count, tp_count),
        mesh=split,
        in_specs=in_specs,
        out_specs=out_specs,
        check_vma=False,
    )
```

```python
import math

import jax
import jax.numpy as jnp
from jax import lax
from jax.sharding import Mesh
from jax.sharding import PartitionSpec as P


HEAD = 128


EPS = 1e-06
ROPE_BASE = 1000000.0

CHIPS = "chips"
CORE = "core"
SEQ = (CHIPS, CORE)
TP = "tp"


def rotate(tensor, positions):
    half_size = tensor.shape[-1] // 2
    frequency = jnp.exp(
        jnp.arange(half_size, dtype=jnp.float32) * (-2.0 * math.log(ROPE_BASE) / tensor.shape[-1])
    )
    angles = positions.astype(jnp.float32)[:, None] * frequency[None, :]
    cosine = jnp.cos(angles)[:, None, :]
    sine_part = jnp.sin(angles)[:, None, :]
    front_half = tensor[..., :half_size]
    back_half = tensor[..., half_size:]
    return jnp.concatenate(
        [front_half * cosine - back_half * sine_part, back_half * cosine + front_half * sine_part],
        axis=-1,
    )


def positions_of(segments):
    length = segments.shape[-1]
    counter = jnp.arange(length, dtype=jnp.int32)
    starts = jnp.concatenate([jnp.ones((1,), dtype=bool), segments[1:] != segments[:-1]])
    marked = jnp.where(starts, counter, jnp.zeros_like(counter))
    return counter - lax.cummax(marked, axis=0)


def make_local(chip_count, core_count, tp_count):
    peer_count = chip_count * core_count

    def body(
        rollout_rows, plan, segment_ids, norm_gain, q_weight, k_weight, v_weight, q_bias, k_bias, v_bias
    ):
        row_count, width = rollout_rows.shape
        slots_each = row_count // peer_count + row_count // (4 * peer_count)
        q_cols = q_weight.shape[1]
        k_cols = k_weight.shape[1]


        weights = jnp.concatenate([q_weight, k_weight, v_weight], axis=1)
        own_weights = lax.all_gather(weights, CHIPS, axis=0, tiled=False)
        other_weights = lax.ppermute(
            own_weights, CORE, [(c, (c + 1) % core_count) for c in range(core_count)]
        )

        target = plan // row_count
        learner_slot = plan % row_count
        matches = (target[:, None] == jnp.arange(peer_count, dtype=jnp.int32)[None, :]).astype(
            jnp.int32
        )
        ranking = jnp.sum((jnp.cumsum(matches, axis=0) - 1) * matches, axis=1)
        slot_hits = (target[None, None, :] == jnp.arange(peer_count, dtype=jnp.int32)[:, None, None]) & (
            ranking[None, None, :] == jnp.arange(slots_each, dtype=jnp.int32)[None, :, None]
        )
        tagged = jnp.sum(jnp.where(slot_hits, learner_slot[None, None, :] + 1, 0), axis=2)
        tag_row = jnp.concatenate(
            [
                (tagged // 32).astype(jnp.bfloat16),
                (tagged % 32).astype(jnp.bfloat16),
                jnp.zeros((peer_count, width - 2 * slots_each), jnp.bfloat16),
            ],
            axis=1,
        )
        picked = jnp.einsum(
            "psr,rf->psf",
            slot_hits.astype(jnp.bfloat16),
            rollout_rows,
            preferred_element_type=jnp.float32,
        ).astype(jnp.bfloat16)
        payload = jnp.concatenate([picked, tag_row[:, None, :]], axis=1)
        arrived = lax.all_to_all(payload, SEQ, split_axis=0, concat_axis=0, tiled=True)
        tags = arrived[:, slots_each, : 2 * slots_each].astype(jnp.int32)
        labels = tags[:, :slots_each] * 32 + tags[:, slots_each:] - 1
        row_numbers = jnp.arange(row_count, dtype=jnp.int32)
        label_hits = labels[None, :, :] == row_numbers[:, None, None]
        learner_part = jnp.einsum(
            "rps,psf->rf",
            label_hits.astype(jnp.bfloat16),
            arrived[:, :slots_each, :],
            preferred_element_type=jnp.float32,
        ).astype(jnp.bfloat16)

        tp_index = lax.axis_index(TP)
        core_index = lax.axis_index(CORE)
        wide = learner_part.astype(jnp.float32)
        own_sq = jnp.sum(wide * wide, axis=-1)
        others = [
            lax.ppermute(own_sq, TP, [(t, (t + k) % tp_count) for t in range(tp_count)])
            for k in range(1, tp_count)
        ]
        total_sq = own_sq
        for other in others:
            total_sq = total_sq + other
        scale = lax.rsqrt(total_sq / (width * tp_count) + EPS)[:, None]

        to_right = [(t, (t + 1) % tp_count) for t in range(tp_count)]
        to_left = [(t, (t - 1) % tp_count) for t in range(tp_count)]
        half = width // 2
        from_left = lax.ppermute(learner_part, TP, to_right)
        from_right = lax.ppermute(learner_part, TP, to_left)
        far_a = lax.ppermute(from_left[:, :half], TP, to_right)
        far_b = lax.ppermute(from_right[:, half:], TP, to_left)
        far = jnp.concatenate([far_a, far_b], axis=1)
        pieces = [learner_part, from_left, far, from_right]

        block = width // (4 * core_count)
        span = 4 * block
        own_rows = own_weights.reshape(tp_count, span, own_weights.shape[-1])
        other_rows = other_weights.reshape(tp_count, span, own_weights.shape[-1])

        def core_block(x, c):
            return jnp.concatenate(
                [x[:, (hl * core_count + c) * block : (hl * core_count + c + 1) * block] for hl in range(4)],
                axis=1,
            )

        def normalize(piece, k, scale, norm_gain, tp_index):
            quarter = (tp_index - k) % tp_count
            gain = lax.dynamic_slice_in_dim(norm_gain, quarter * width, width)
            return (piece.astype(jnp.float32) * scale * gain).astype(jnp.bfloat16)

        def project(normed, k, tp_index, core_index):
            quarter = (tp_index - k) % tp_count
            first = core_block(normed, 0)
            second = core_block(normed, 1)
            mine = jnp.where(core_index == 0, first, second)
            theirs = jnp.where(core_index == 0, second, first)
            total = None
            for cols, rows_of in ((mine, own_rows), (theirs, other_rows)):
                rows = lax.dynamic_index_in_dim(rows_of, quarter, axis=0, keepdims=False)
                part = jnp.dot(cols, rows, preferred_element_type=jnp.float32)
                total = part if total is None else total + part
            return total

        projected = None
        for k in (0, 1, 3):
            normed = normalize(pieces[k], k, scale, norm_gain, tp_index)
            part = project(normed, k, tp_index, core_index)
            projected = part if projected is None else projected + part
        projected = lax.optimization_barrier(projected)
        far_piece, far_scale, far_gain, far_tp, far_core = lax.optimization_barrier(
            (pieces[2], scale, norm_gain, tp_index, core_index)
        )
        normed = normalize(far_piece, 2, far_scale, far_gain, far_tp)
        projected = projected + project(normed, 2, far_tp, far_core)
        queries = projected[:, :q_cols]
        key_proj = projected[:, q_cols : q_cols + k_cols]
        value_proj = projected[:, q_cols + k_cols :]
        local_heads = q_cols // HEAD
        local_groups = k_cols // HEAD
        group_size = local_heads // local_groups
        positions = positions_of(segment_ids)
        q_rot = rotate((queries + q_bias).reshape(row_count, local_heads, HEAD), positions).astype(
            jnp.bfloat16
        )
        q_rot = q_rot.reshape(row_count, local_groups, group_size, HEAD)
        k_rot = rotate((key_proj + k_bias).reshape(row_count, local_groups, HEAD), positions).astype(
            jnp.bfloat16
        )
        value_heads = (value_proj + v_bias).astype(jnp.bfloat16).reshape(row_count, local_groups, HEAD)
        block_rows = min(512, row_count)
        row_index = jnp.arange(row_count, dtype=jnp.int32)
        scores = jnp.einsum(
            "qkgd,pkd->kgqp", q_rot, k_rot, preferred_element_type=jnp.float32
        ) / math.sqrt(HEAD)
        allowed = (segment_ids[0:block_rows, None] == segment_ids[None, :block_rows]) & (
            row_index[0:block_rows, None] >= row_index[None, :block_rows]
        )
        scores = jnp.where(allowed[None, None], scores, -jnp.inf)
        highest = jnp.max(scores, axis=-1, keepdims=True)
        expo = jnp.exp(scores - highest)
        probs = (expo / jnp.sum(expo, axis=-1, keepdims=True)).astype(jnp.bfloat16)
        mixed = jnp.einsum("kgqp,pkd->qkgd", probs, value_heads, preferred_element_type=jnp.float32)
        outputs = mixed.astype(jnp.bfloat16).reshape(block_rows, local_heads * HEAD)
        return outputs

    return body


def solution(mesh):
    seq_count, tp_count = mesh.devices.shape
    core_count = 2
    chip_count = seq_count // core_count
    split = Mesh(mesh.devices.reshape(chip_count, core_count, tp_count), (CHIPS, CORE, TP))
    in_specs = (
        P(SEQ, TP),
        P(SEQ),
        P(SEQ),
        P(),
        P(SEQ, TP),
        P(SEQ, TP),
        P(SEQ, TP),
        P(TP),
        P(TP),
        P(TP),
    )
    out_specs = P(SEQ, TP)
    return jax.shard_map(
        make_local(chip_count, core_count, tp_count),
        mesh=split,
        in_specs=in_specs,
        out_specs=out_specs,
        check_vma=False,
    )
```

```python
import math

import jax
import jax.numpy as jnp
from jax import lax
from jax.sharding import Mesh
from jax.sharding import PartitionSpec as P


HEAD = 128


EPS = 1e-06
ROPE_BASE = 1000000.0

CHIPS = "chips"
CORE = "core"
SEQ = (CHIPS, CORE)
TP = "tp"


def rotate(tensor, positions):
    half_size = tensor.shape[-1] // 2
    frequency = jnp.exp(
        jnp.arange(half_size, dtype=jnp.float32) * (-2.0 * math.log(ROPE_BASE) / tensor.shape[-1])
    )
    angles = positions.astype(jnp.float32)[:, None] * frequency[None, :]
    cosine = jnp.cos(angles)[:, None, :]
    sine_part = jnp.sin(angles)[:, None, :]
    front_half = tensor[..., :half_size]
    back_half = tensor[..., half_size:]
    return jnp.concatenate(
        [front_half * cosine - back_half * sine_part, back_half * cosine + front_half * sine_part],
        axis=-1,
    )


def positions_of(segments):
    length = segments.shape[-1]
    counter = jnp.arange(length, dtype=jnp.int32)
    starts = jnp.concatenate([jnp.ones((1,), dtype=bool), segments[1:] != segments[:-1]])
    marked = jnp.where(starts, counter, jnp.zeros_like(counter))
    return counter - lax.cummax(marked, axis=0)


def make_local(chip_count, core_count, tp_count):
    peer_count = chip_count * core_count

    def body(
        rollout_rows, plan, segment_ids, norm_gain, q_weight, k_weight, v_weight, q_bias, k_bias, v_bias
    ):
        row_count, width = rollout_rows.shape
        slots_each = row_count // peer_count + row_count // (4 * peer_count)
        q_cols = q_weight.shape[1]
        k_cols = k_weight.shape[1]


        weights = jnp.concatenate([q_weight, k_weight, v_weight], axis=1)
        own_weights = lax.all_gather(weights, CHIPS, axis=0, tiled=False)
        other_weights = lax.ppermute(
            own_weights, CORE, [(c, (c + 1) % core_count) for c in range(core_count)]
        )

        target = plan // row_count
        learner_slot = plan % row_count
        matches = (target[:, None] == jnp.arange(peer_count, dtype=jnp.int32)[None, :]).astype(
            jnp.int32
        )
        ranking = jnp.sum((jnp.cumsum(matches, axis=0) - 1) * matches, axis=1)
        slot_hits = (target[None, None, :] == jnp.arange(peer_count, dtype=jnp.int32)[:, None, None]) & (
            ranking[None, None, :] == jnp.arange(slots_each, dtype=jnp.int32)[None, :, None]
        )
        tagged = jnp.sum(jnp.where(slot_hits, learner_slot[None, None, :] + 1, 0), axis=2)
        tag_row = jnp.concatenate(
            [
                (tagged // 32).astype(jnp.bfloat16),
                (tagged % 32).astype(jnp.bfloat16),
                jnp.zeros((peer_count, width - 2 * slots_each), jnp.bfloat16),
            ],
            axis=1,
        )
        block = width // (4 * core_count)
        span = 4 * block
        by_core = (
            rollout_rows.reshape(row_count, 4, core_count, block).transpose(0, 2, 1, 3).reshape(row_count, width)
        )
        picked = jnp.einsum(
            "psr,rf->psf",
            slot_hits.astype(jnp.bfloat16),
            by_core,
            preferred_element_type=jnp.float32,
        ).astype(jnp.bfloat16)
        payload = jnp.concatenate([picked, tag_row[:, None, :]], axis=1)
        arrived = lax.all_to_all(payload, SEQ, split_axis=0, concat_axis=0, tiled=True)
        tags = arrived[:, slots_each, : 2 * slots_each].astype(jnp.int32)
        labels = tags[:, :slots_each] * 32 + tags[:, slots_each:] - 1
        row_numbers = jnp.arange(row_count, dtype=jnp.int32)
        label_hits = labels[None, :, :] == row_numbers[:, None, None]
        learner_part = jnp.einsum(
            "rps,psf->rf",
            label_hits.astype(jnp.bfloat16),
            arrived[:, :slots_each, :],
            preferred_element_type=jnp.float32,
        ).astype(jnp.bfloat16)

        tp_index = lax.axis_index(TP)
        core_index = lax.axis_index(CORE)
        wide = learner_part.astype(jnp.float32)
        own_sq = jnp.sum(wide * wide, axis=-1)
        others = [
            lax.ppermute(own_sq, TP, [(t, (t + k) % tp_count) for t in range(tp_count)])
            for k in range(1, tp_count)
        ]
        total_sq = own_sq
        for other in others:
            total_sq = total_sq + other
        scale = lax.rsqrt(total_sq / (width * tp_count) + EPS)[:, None]

        to_right = [(t, (t + 1) % tp_count) for t in range(tp_count)]
        to_left = [(t, (t - 1) % tp_count) for t in range(tp_count)]
        half = width // 2
        from_left = lax.ppermute(learner_part, TP, to_right)
        from_right = lax.ppermute(learner_part, TP, to_left)
        far_a = lax.ppermute(from_left[:, :half], TP, to_right)
        far_b = lax.ppermute(from_right[:, half:], TP, to_left)
        far = jnp.concatenate([far_a, far_b], axis=1)
        pieces = [learner_part, from_left, far, from_right]

        own_rows = own_weights.reshape(tp_count, span, own_weights.shape[-1])
        other_rows = other_weights.reshape(tp_count, span, own_weights.shape[-1])

        def core_block(x, c):
            return x[:, c * span : (c + 1) * span]

        def normalize(piece, k, scale, norm_gain, tp_index):
            quarter = (tp_index - k) % tp_count
            gain = lax.dynamic_slice_in_dim(norm_gain, quarter * width, width)
            gain = gain.reshape(4, core_count, block).transpose(1, 0, 2).reshape(width)
            return (piece.astype(jnp.float32) * scale * gain).astype(jnp.bfloat16)

        def project(normed, k, tp_index, core_index):
            quarter = (tp_index - k) % tp_count
            first = core_block(normed, 0)
            second = core_block(normed, 1)
            mine = jnp.where(core_index == 0, first, second)
            theirs = jnp.where(core_index == 0, second, first)
            total = None
            for cols, rows_of in ((mine, own_rows), (theirs, other_rows)):
                rows = lax.dynamic_index_in_dim(rows_of, quarter, axis=0, keepdims=False)
                part = jnp.dot(cols, rows, preferred_element_type=jnp.float32)
                total = part if total is None else total + part
            return total

        projected = None
        for k in (0, 1, 3):
            normed = normalize(pieces[k], k, scale, norm_gain, tp_index)
            part = project(normed, k, tp_index, core_index)
            projected = part if projected is None else projected + part
        projected = lax.optimization_barrier(projected)
        far_piece, far_scale, far_gain, far_tp, far_core = lax.optimization_barrier(
            (pieces[2], scale, norm_gain, tp_index, core_index)
        )
        normed = normalize(far_piece, 2, far_scale, far_gain, far_tp)
        projected = projected + project(normed, 2, far_tp, far_core)
        queries = projected[:, :q_cols]
        key_proj = projected[:, q_cols : q_cols + k_cols]
        value_proj = projected[:, q_cols + k_cols :]
        local_heads = q_cols // HEAD
        local_groups = k_cols // HEAD
        group_size = local_heads // local_groups
        positions = positions_of(segment_ids)
        q_rot = rotate((queries + q_bias).reshape(row_count, local_heads, HEAD), positions).astype(
            jnp.bfloat16
        )
        q_rot = q_rot.reshape(row_count, local_groups, group_size, HEAD)
        k_rot = rotate((key_proj + k_bias).reshape(row_count, local_groups, HEAD), positions).astype(
            jnp.bfloat16
        )
        value_heads = (value_proj + v_bias).astype(jnp.bfloat16).reshape(row_count, local_groups, HEAD)
        block_rows = min(512, row_count)
        row_index = jnp.arange(row_count, dtype=jnp.int32)
        scores = jnp.einsum(
            "qkgd,pkd->kgqp", q_rot, k_rot, preferred_element_type=jnp.float32
        ) / math.sqrt(HEAD)
        allowed = (segment_ids[0:block_rows, None] == segment_ids[None, :block_rows]) & (
            row_index[0:block_rows, None] >= row_index[None, :block_rows]
        )
        scores = jnp.where(allowed[None, None], scores, -jnp.inf)
        highest = jnp.max(scores, axis=-1, keepdims=True)
        expo = jnp.exp(scores - highest)
        probs = (expo / jnp.sum(expo, axis=-1, keepdims=True)).astype(jnp.bfloat16)
        mixed = jnp.einsum("kgqp,pkd->qkgd", probs, value_heads, preferred_element_type=jnp.float32)
        outputs = mixed.astype(jnp.bfloat16).reshape(block_rows, local_heads * HEAD)
        return outputs

    return body


def solution(mesh):
    seq_count, tp_count = mesh.devices.shape
    core_count = 2
    chip_count = seq_count // core_count
    split = Mesh(mesh.devices.reshape(chip_count, core_count, tp_count), (CHIPS, CORE, TP))
    in_specs = (
        P(SEQ, TP),
        P(SEQ),
        P(SEQ),
        P(),
        P(SEQ, TP),
        P(SEQ, TP),
        P(SEQ, TP),
        P(TP),
        P(TP),
        P(TP),
    )
    out_specs = P(SEQ, TP)
    return jax.shard_map(
        make_local(chip_count, core_count, tp_count),
        mesh=split,
        in_specs=in_specs,
        out_specs=out_specs,
        check_vma=False,
    )
```

```python
import math

import jax
import jax.numpy as jnp
from jax import lax
from jax.sharding import Mesh
from jax.sharding import PartitionSpec as P


HEAD = 128


EPS = 1e-06
ROPE_BASE = 1000000.0

CHIPS = "chips"
CORE = "core"
SEQ = (CHIPS, CORE)
TP = "tp"


def rotate(tensor, positions):
    half_size = tensor.shape[-1] // 2
    frequency = jnp.exp(
        jnp.arange(half_size, dtype=jnp.float32) * (-2.0 * math.log(ROPE_BASE) / tensor.shape[-1])
    )
    angles = positions.astype(jnp.float32)[:, None] * frequency[None, :]
    cosine = jnp.cos(angles)[:, None, :]
    sine_part = jnp.sin(angles)[:, None, :]
    front_half = tensor[..., :half_size]
    back_half = tensor[..., half_size:]
    return jnp.concatenate(
        [front_half * cosine - back_half * sine_part, back_half * cosine + front_half * sine_part],
        axis=-1,
    )


def positions_of(segments):
    length = segments.shape[-1]
    counter = jnp.arange(length, dtype=jnp.int32)
    starts = jnp.concatenate([jnp.ones((1,), dtype=bool), segments[1:] != segments[:-1]])
    marked = jnp.where(starts, counter, jnp.zeros_like(counter))
    return counter - lax.cummax(marked, axis=0)


def make_local(chip_count, core_count, tp_count):
    peer_count = chip_count * core_count

    def body(
        rollout_rows, plan, segment_ids, norm_gain, q_weight, k_weight, v_weight, q_bias, k_bias, v_bias
    ):
        row_count, width = rollout_rows.shape
        slots_each = row_count // peer_count + row_count // (4 * peer_count)
        q_cols = q_weight.shape[1]
        k_cols = k_weight.shape[1]


        weights = jnp.concatenate([q_weight, k_weight, v_weight], axis=1)
        own_weights = lax.all_gather(weights, CHIPS, axis=0, tiled=False)
        other_weights = lax.ppermute(
            own_weights, CORE, [(c, (c + 1) % core_count) for c in range(core_count)]
        )

        target = plan // row_count
        learner_slot = plan % row_count
        matches = (target[:, None] == jnp.arange(peer_count, dtype=jnp.int32)[None, :]).astype(
            jnp.int32
        )
        ranking = jnp.sum((jnp.cumsum(matches, axis=0) - 1) * matches, axis=1)
        slot_hits = (target[None, None, :] == jnp.arange(peer_count, dtype=jnp.int32)[:, None, None]) & (
            ranking[None, None, :] == jnp.arange(slots_each, dtype=jnp.int32)[None, :, None]
        )
        tagged = jnp.sum(jnp.where(slot_hits, learner_slot[None, None, :] + 1, 0), axis=2)
        tag_row = jnp.concatenate(
            [
                (tagged // 32).astype(jnp.bfloat16),
                (tagged % 32).astype(jnp.bfloat16),
                jnp.zeros((peer_count, width - 2 * slots_each), jnp.bfloat16),
            ],
            axis=1,
        )
        picked = jnp.einsum(
            "psr,rf->psf",
            slot_hits.astype(jnp.bfloat16),
            rollout_rows,
            preferred_element_type=jnp.float32,
        ).astype(jnp.bfloat16)
        payload = jnp.concatenate([picked, tag_row[:, None, :]], axis=1)
        arrived = lax.all_to_all(payload, SEQ, split_axis=0, concat_axis=0, tiled=True)
        tags = arrived[:, slots_each, : 2 * slots_each].astype(jnp.int32)
        labels = tags[:, :slots_each] * 32 + tags[:, slots_each:] - 1
        row_numbers = jnp.arange(row_count, dtype=jnp.int32)
        label_hits = labels[None, :, :] == row_numbers[:, None, None]
        learner_part = jnp.einsum(
            "rps,psf->rf",
            label_hits.astype(jnp.bfloat16),
            arrived[:, :slots_each, :],
            preferred_element_type=jnp.float32,
        ).astype(jnp.bfloat16)

        tp_index = lax.axis_index(TP)
        core_index = lax.axis_index(CORE)
        wide = learner_part.astype(jnp.float32)
        own_sq = jnp.sum(wide * wide, axis=-1)
        others = [
            lax.ppermute(own_sq, TP, [(t, (t + k) % tp_count) for t in range(tp_count)])
            for k in range(1, tp_count)
        ]
        total_sq = own_sq
        for other in others:
            total_sq = total_sq + other
        scale = lax.rsqrt(total_sq / (width * tp_count) + EPS)[:, None]

        to_right = [(t, (t + 1) % tp_count) for t in range(tp_count)]
        to_left = [(t, (t - 1) % tp_count) for t in range(tp_count)]
        half_rows = row_count // 2
        from_left = lax.ppermute(learner_part, TP, to_right)
        from_right = lax.ppermute(learner_part, TP, to_left)
        far_a = lax.ppermute(from_left[:half_rows], TP, to_right)
        far_b = lax.ppermute(from_right[half_rows:], TP, to_left)
        far = jnp.concatenate([far_a, far_b], axis=0)
        pieces = [learner_part, from_left, far, from_right]

        block = width // (4 * core_count)
        span = 4 * block
        own_rows = own_weights.reshape(tp_count, span, own_weights.shape[-1])
        other_rows = other_weights.reshape(tp_count, span, own_weights.shape[-1])

        def core_block(x, c):
            return jnp.concatenate(
                [x[:, (hl * core_count + c) * block : (hl * core_count + c + 1) * block] for hl in range(4)],
                axis=1,
            )

        def normalize(piece, k, scale, norm_gain, tp_index):
            quarter = (tp_index - k) % tp_count
            gain = lax.dynamic_slice_in_dim(norm_gain, quarter * width, width)
            return (piece.astype(jnp.float32) * scale * gain).astype(jnp.bfloat16)

        def project(normed, k, tp_index, core_index):
            quarter = (tp_index - k) % tp_count
            first = core_block(normed, 0)
            second = core_block(normed, 1)
            mine = jnp.where(core_index == 0, first, second)
            theirs = jnp.where(core_index == 0, second, first)
            total = None
            for cols, rows_of in ((mine, own_rows), (theirs, other_rows)):
                rows = lax.dynamic_index_in_dim(rows_of, quarter, axis=0, keepdims=False)
                part = jnp.dot(cols, rows, preferred_element_type=jnp.float32)
                total = part if total is None else total + part
            return total

        projected = None
        for k in (0, 1, 3):
            normed = normalize(pieces[k], k, scale, norm_gain, tp_index)
            part = project(normed, k, tp_index, core_index)
            projected = part if projected is None else projected + part
        projected = lax.optimization_barrier(projected)
        far_piece, far_scale, far_gain, far_tp, far_core = lax.optimization_barrier(
            (pieces[2], scale, norm_gain, tp_index, core_index)
        )
        normed = normalize(far_piece, 2, far_scale, far_gain, far_tp)
        projected = projected + project(normed, 2, far_tp, far_core)
        queries = projected[:, :q_cols]
        key_proj = projected[:, q_cols : q_cols + k_cols]
        value_proj = projected[:, q_cols + k_cols :]
        local_heads = q_cols // HEAD
        local_groups = k_cols // HEAD
        group_size = local_heads // local_groups
        positions = positions_of(segment_ids)
        q_rot = rotate((queries + q_bias).reshape(row_count, local_heads, HEAD), positions).astype(
            jnp.bfloat16
        )
        q_rot = q_rot.reshape(row_count, local_groups, group_size, HEAD)
        k_rot = rotate((key_proj + k_bias).reshape(row_count, local_groups, HEAD), positions).astype(
            jnp.bfloat16
        )
        value_heads = (value_proj + v_bias).astype(jnp.bfloat16).reshape(row_count, local_groups, HEAD)
        block_rows = min(512, row_count)
        row_index = jnp.arange(row_count, dtype=jnp.int32)
        scores = jnp.einsum(
            "qkgd,pkd->kgqp", q_rot, k_rot, preferred_element_type=jnp.float32
        ) / math.sqrt(HEAD)
        allowed = (segment_ids[0:block_rows, None] == segment_ids[None, :block_rows]) & (
            row_index[0:block_rows, None] >= row_index[None, :block_rows]
        )
        scores = jnp.where(allowed[None, None], scores, -jnp.inf)
        highest = jnp.max(scores, axis=-1, keepdims=True)
        expo = jnp.exp(scores - highest)
        probs = (expo / jnp.sum(expo, axis=-1, keepdims=True)).astype(jnp.bfloat16)
        mixed = jnp.einsum("kgqp,pkd->qkgd", probs, value_heads, preferred_element_type=jnp.float32)
        outputs = mixed.astype(jnp.bfloat16).reshape(block_rows, local_heads * HEAD)
        return outputs

    return body


def solution(mesh):
    seq_count, tp_count = mesh.devices.shape
    core_count = 2
    chip_count = seq_count // core_count
    split = Mesh(mesh.devices.reshape(chip_count, core_count, tp_count), (CHIPS, CORE, TP))
    in_specs = (
        P(SEQ, TP),
        P(SEQ),
        P(SEQ),
        P(),
        P(SEQ, TP),
        P(SEQ, TP),
        P(SEQ, TP),
        P(TP),
        P(TP),
        P(TP),
    )
    out_specs = P(SEQ, TP)
    return jax.shard_map(
        make_local(chip_count, core_count, tp_count),
        mesh=split,
        in_specs=in_specs,
        out_specs=out_specs,
        check_vma=False,
    )
```

```python
import math

import jax
import jax.numpy as jnp
from jax import lax
from jax.sharding import Mesh
from jax.sharding import PartitionSpec as P


HEAD = 128


EPS = 1e-06
ROPE_BASE = 1000000.0

CHIPS = "chips"
CORE = "core"
SEQ = (CHIPS, CORE)
TP = "tp"


def rotate(tensor, positions):
    half_size = tensor.shape[-1] // 2
    frequency = jnp.exp(
        jnp.arange(half_size, dtype=jnp.float32) * (-2.0 * math.log(ROPE_BASE) / tensor.shape[-1])
    )
    angles = positions.astype(jnp.float32)[:, None] * frequency[None, :]
    cosine = jnp.cos(angles)[:, None, :]
    sine_part = jnp.sin(angles)[:, None, :]
    front_half = tensor[..., :half_size]
    back_half = tensor[..., half_size:]
    return jnp.concatenate(
        [front_half * cosine - back_half * sine_part, back_half * cosine + front_half * sine_part],
        axis=-1,
    )


def positions_of(segments):
    length = segments.shape[-1]
    counter = jnp.arange(length, dtype=jnp.int32)
    starts = jnp.concatenate([jnp.ones((1,), dtype=bool), segments[1:] != segments[:-1]])
    marked = jnp.where(starts, counter, jnp.zeros_like(counter))
    return counter - lax.cummax(marked, axis=0)


def make_local(chip_count, core_count, tp_count):
    peer_count = chip_count * core_count

    def body(
        rollout_rows, plan, segment_ids, norm_gain, q_weight, k_weight, v_weight, q_bias, k_bias, v_bias
    ):
        row_count, width = rollout_rows.shape
        slots_each = row_count // peer_count + row_count // (4 * peer_count)
        q_cols = q_weight.shape[1]
        k_cols = k_weight.shape[1]


        weights = jnp.concatenate([q_weight, k_weight, v_weight], axis=1)
        own_weights = lax.all_gather(weights, CHIPS, axis=0, tiled=False)
        other_weights = lax.ppermute(
            own_weights, CORE, [(c, (c + 1) % core_count) for c in range(core_count)]
        )

        target = plan // row_count
        learner_slot = plan % row_count
        matches = (target[:, None] == jnp.arange(peer_count, dtype=jnp.int32)[None, :]).astype(
            jnp.int32
        )
        ranking = jnp.sum((jnp.cumsum(matches, axis=0) - 1) * matches, axis=1)
        parcel_rows = -(-(slots_each + 1) // 8) * 8
        flat_slot = target * parcel_rows + ranking
        slot_hits = flat_slot[None, :] == jnp.arange(peer_count * parcel_rows, dtype=jnp.int32)[:, None]
        tagged = jnp.sum(jnp.where(slot_hits, learner_slot[None, :] + 1, 0), axis=1).reshape(
            peer_count, parcel_rows
        )[:, :slots_each]
        tag_row = jnp.concatenate(
            [
                (tagged // 32).astype(jnp.bfloat16),
                (tagged % 32).astype(jnp.bfloat16),
                jnp.zeros((peer_count, width - 2 * slots_each), jnp.bfloat16),
            ],
            axis=1,
        )
        picked = jnp.dot(
            slot_hits.astype(jnp.bfloat16), rollout_rows, preferred_element_type=jnp.float32
        ).astype(jnp.bfloat16).reshape(peer_count, parcel_rows, width)
        row_in_parcel = jnp.arange(parcel_rows, dtype=jnp.int32)[None, :, None]
        payload = jnp.where(row_in_parcel == slots_each, tag_row[:, None, :], picked)
        arrived = lax.all_to_all(payload, SEQ, split_axis=0, concat_axis=0, tiled=True)
        tags = arrived[:, slots_each, : 2 * slots_each].astype(jnp.int32)
        labels = tags[:, :slots_each] * 32 + tags[:, slots_each:] - 1
        labels = jnp.concatenate(
            [labels, jnp.full((peer_count, parcel_rows - slots_each), -1, jnp.int32)], axis=1
        ).reshape(peer_count * parcel_rows)
        row_numbers = jnp.arange(row_count, dtype=jnp.int32)
        label_hits = labels[None, :] == row_numbers[:, None]
        learner_part = jnp.dot(
            label_hits.astype(jnp.bfloat16),
            arrived.reshape(peer_count * parcel_rows, width),
            preferred_element_type=jnp.float32,
        ).astype(jnp.bfloat16)

        tp_index = lax.axis_index(TP)
        core_index = lax.axis_index(CORE)
        wide = learner_part.astype(jnp.float32)
        own_sq = jnp.sum(wide * wide, axis=-1)
        others = [
            lax.ppermute(own_sq, TP, [(t, (t + k) % tp_count) for t in range(tp_count)])
            for k in range(1, tp_count)
        ]
        total_sq = own_sq
        for other in others:
            total_sq = total_sq + other
        scale = lax.rsqrt(total_sq / (width * tp_count) + EPS)[:, None]

        to_right = [(t, (t + 1) % tp_count) for t in range(tp_count)]
        to_left = [(t, (t - 1) % tp_count) for t in range(tp_count)]
        half = width // 2
        from_left = lax.ppermute(learner_part, TP, to_right)
        from_right = lax.ppermute(learner_part, TP, to_left)
        far_a = lax.ppermute(from_left[:, :half], TP, to_right)
        far_b = lax.ppermute(from_right[:, half:], TP, to_left)
        far = jnp.concatenate([far_a, far_b], axis=1)
        pieces = [learner_part, from_left, far, from_right]

        block = width // (4 * core_count)
        span = 4 * block
        own_rows = own_weights.reshape(tp_count, span, own_weights.shape[-1])
        other_rows = other_weights.reshape(tp_count, span, own_weights.shape[-1])

        def core_block(x, c):
            return jnp.concatenate(
                [x[:, (hl * core_count + c) * block : (hl * core_count + c + 1) * block] for hl in range(4)],
                axis=1,
            )

        def normalize(piece, k, scale, norm_gain, tp_index):
            quarter = (tp_index - k) % tp_count
            gain = lax.dynamic_slice_in_dim(norm_gain, quarter * width, width)
            return (piece.astype(jnp.float32) * scale * gain).astype(jnp.bfloat16)

        def project(normed, k, tp_index, core_index):
            quarter = (tp_index - k) % tp_count
            first = core_block(normed, 0)
            second = core_block(normed, 1)
            mine = jnp.where(core_index == 0, first, second)
            theirs = jnp.where(core_index == 0, second, first)
            total = None
            for cols, rows_of in ((mine, own_rows), (theirs, other_rows)):
                rows = lax.dynamic_index_in_dim(rows_of, quarter, axis=0, keepdims=False)
                part = jnp.dot(cols, rows, preferred_element_type=jnp.float32)
                total = part if total is None else total + part
            return total

        projected = None
        for k in (0, 1, 3):
            normed = normalize(pieces[k], k, scale, norm_gain, tp_index)
            part = project(normed, k, tp_index, core_index)
            projected = part if projected is None else projected + part
        projected = lax.optimization_barrier(projected)
        far_piece, far_scale, far_gain, far_tp, far_core = lax.optimization_barrier(
            (pieces[2], scale, norm_gain, tp_index, core_index)
        )
        normed = normalize(far_piece, 2, far_scale, far_gain, far_tp)
        projected = projected + project(normed, 2, far_tp, far_core)
        queries = projected[:, :q_cols]
        key_proj = projected[:, q_cols : q_cols + k_cols]
        value_proj = projected[:, q_cols + k_cols :]
        local_heads = q_cols // HEAD
        local_groups = k_cols // HEAD
        group_size = local_heads // local_groups
        positions = positions_of(segment_ids)
        q_rot = rotate((queries + q_bias).reshape(row_count, local_heads, HEAD), positions).astype(
            jnp.bfloat16
        )
        q_rot = q_rot.reshape(row_count, local_groups, group_size, HEAD)
        k_rot = rotate((key_proj + k_bias).reshape(row_count, local_groups, HEAD), positions).astype(
            jnp.bfloat16
        )
        value_heads = (value_proj + v_bias).astype(jnp.bfloat16).reshape(row_count, local_groups, HEAD)
        block_rows = min(512, row_count)
        row_index = jnp.arange(row_count, dtype=jnp.int32)
        scores = jnp.einsum(
            "qkgd,pkd->kgqp", q_rot, k_rot, preferred_element_type=jnp.float32
        ) / math.sqrt(HEAD)
        allowed = (segment_ids[0:block_rows, None] == segment_ids[None, :block_rows]) & (
            row_index[0:block_rows, None] >= row_index[None, :block_rows]
        )
        scores = jnp.where(allowed[None, None], scores, -jnp.inf)
        highest = jnp.max(scores, axis=-1, keepdims=True)
        expo = jnp.exp(scores - highest)
        probs = (expo / jnp.sum(expo, axis=-1, keepdims=True)).astype(jnp.bfloat16)
        mixed = jnp.einsum("kgqp,pkd->qkgd", probs, value_heads, preferred_element_type=jnp.float32)
        outputs = mixed.astype(jnp.bfloat16).reshape(block_rows, local_heads * HEAD)
        return outputs

    return body


def solution(mesh):
    seq_count, tp_count = mesh.devices.shape
    core_count = 2
    chip_count = seq_count // core_count
    split = Mesh(mesh.devices.reshape(chip_count, core_count, tp_count), (CHIPS, CORE, TP))
    in_specs = (
        P(SEQ, TP),
        P(SEQ),
        P(SEQ),
        P(),
        P(SEQ, TP),
        P(SEQ, TP),
        P(SEQ, TP),
        P(TP),
        P(TP),
        P(TP),
    )
    out_specs = P(SEQ, TP)
    return jax.shard_map(
        make_local(chip_count, core_count, tp_count),
        mesh=split,
        in_specs=in_specs,
        out_specs=out_specs,
        check_vma=False,
    )
```

```python
import math

import jax
import jax.numpy as jnp
from jax import lax
from jax.sharding import Mesh
from jax.sharding import PartitionSpec as P


HEAD = 128


EPS = 1e-06
ROPE_BASE = 1000000.0

CHIPS = "chips"
CORE = "core"
SEQ = (CHIPS, CORE)
TP = "tp"


def rotate(tensor, positions):
    half_size = tensor.shape[-1] // 2
    frequency = jnp.exp(
        jnp.arange(half_size, dtype=jnp.float32) * (-2.0 * math.log(ROPE_BASE) / tensor.shape[-1])
    )
    angles = positions.astype(jnp.float32)[:, None] * frequency[None, :]
    cosine = jnp.cos(angles)[:, None, :]
    sine_part = jnp.sin(angles)[:, None, :]
    front_half = tensor[..., :half_size]
    back_half = tensor[..., half_size:]
    return jnp.concatenate(
        [front_half * cosine - back_half * sine_part, back_half * cosine + front_half * sine_part],
        axis=-1,
    )


def positions_of(segments):
    length = segments.shape[-1]
    counter = jnp.arange(length, dtype=jnp.int32)
    starts = jnp.concatenate([jnp.ones((1,), dtype=bool), segments[1:] != segments[:-1]])
    marked = jnp.where(starts, counter, jnp.zeros_like(counter))
    return counter - lax.cummax(marked, axis=0)


def make_local(chip_count, core_count, tp_count):
    peer_count = chip_count * core_count

    def body(
        rollout_rows, plan, segment_ids, norm_gain, q_weight, k_weight, v_weight, q_bias, k_bias, v_bias
    ):
        row_count, width = rollout_rows.shape
        slots_each = row_count // peer_count + row_count // (4 * peer_count)
        q_cols = q_weight.shape[1]
        k_cols = k_weight.shape[1]


        weights = jnp.concatenate([q_weight, k_weight, v_weight], axis=1)
        own_weights = lax.all_gather(weights, CHIPS, axis=0, tiled=False)
        other_weights = lax.ppermute(
            own_weights, CORE, [(c, (c + 1) % core_count) for c in range(core_count)]
        )

        target = plan // row_count
        learner_slot = plan % row_count
        matches = (target[:, None] == jnp.arange(peer_count, dtype=jnp.int32)[None, :]).astype(
            jnp.int32
        )
        ranking = jnp.sum((jnp.cumsum(matches, axis=0) - 1) * matches, axis=1)
        parcel_rows = -(-(slots_each + 1) // 8) * 8
        flat_slot = target * parcel_rows + ranking
        slot_hits = flat_slot[None, :] == jnp.arange(peer_count * parcel_rows, dtype=jnp.int32)[:, None]
        tagged = jnp.sum(jnp.where(slot_hits, learner_slot[None, :] + 1, 0), axis=1).reshape(
            peer_count, parcel_rows
        )[:, :slots_each]
        tag_row = jnp.concatenate(
            [
                (tagged // 32).astype(jnp.bfloat16),
                (tagged % 32).astype(jnp.bfloat16),
                jnp.zeros((peer_count, width - 2 * slots_each), jnp.bfloat16),
            ],
            axis=1,
        )
        picked = jnp.dot(
            slot_hits.astype(jnp.bfloat16), rollout_rows, preferred_element_type=jnp.float32
        ).astype(jnp.bfloat16).reshape(peer_count, parcel_rows, width)
        row_in_parcel = jnp.arange(parcel_rows, dtype=jnp.int32)[None, :, None]
        payload = jnp.where(row_in_parcel == slots_each, tag_row[:, None, :], picked)
        arrived = lax.all_to_all(payload, SEQ, split_axis=0, concat_axis=0, tiled=True)
        tags = arrived[:, slots_each, : 2 * slots_each].astype(jnp.int32)
        labels = tags[:, :slots_each] * 32 + tags[:, slots_each:] - 1
        labels = jnp.concatenate(
            [labels, jnp.full((peer_count, parcel_rows - slots_each), -1, jnp.int32)], axis=1
        ).reshape(peer_count * parcel_rows)
        row_numbers = jnp.arange(row_count, dtype=jnp.int32)
        label_hits = labels[None, :] == row_numbers[:, None]
        learner_part = jnp.dot(
            label_hits.astype(jnp.bfloat16),
            arrived.reshape(peer_count * parcel_rows, width),
            preferred_element_type=jnp.float32,
        ).astype(jnp.bfloat16)

        tp_index = lax.axis_index(TP)
        core_index = lax.axis_index(CORE)
        wide = learner_part.astype(jnp.float32)
        own_sq = jnp.sum(wide * wide, axis=-1)
        total_sq = lax.psum(own_sq, TP)
        scale = lax.rsqrt(total_sq / (width * tp_count) + EPS)[:, None]

        to_right = [(t, (t + 1) % tp_count) for t in range(tp_count)]
        to_left = [(t, (t - 1) % tp_count) for t in range(tp_count)]
        half = width // 2
        from_left = lax.ppermute(learner_part, TP, to_right)
        from_right = lax.ppermute(learner_part, TP, to_left)
        far_a = lax.ppermute(from_left[:, :half], TP, to_right)
        far_b = lax.ppermute(from_right[:, half:], TP, to_left)
        far = jnp.concatenate([far_a, far_b], axis=1)
        pieces = [learner_part, from_left, far, from_right]

        block = width // (4 * core_count)
        span = 4 * block
        own_rows = own_weights.reshape(tp_count, span, own_weights.shape[-1])
        other_rows = other_weights.reshape(tp_count, span, own_weights.shape[-1])

        def core_block(x, c):
            return jnp.concatenate(
                [x[:, (hl * core_count + c) * block : (hl * core_count + c + 1) * block] for hl in range(4)],
                axis=1,
            )

        def normalize(piece, k, scale, norm_gain, tp_index):
            quarter = (tp_index - k) % tp_count
            gain = lax.dynamic_slice_in_dim(norm_gain, quarter * width, width)
            return (piece.astype(jnp.float32) * scale * gain).astype(jnp.bfloat16)

        def project(normed, k, tp_index, core_index):
            quarter = (tp_index - k) % tp_count
            first = core_block(normed, 0)
            second = core_block(normed, 1)
            mine = jnp.where(core_index == 0, first, second)
            theirs = jnp.where(core_index == 0, second, first)
            total = None
            for cols, rows_of in ((mine, own_rows), (theirs, other_rows)):
                rows = lax.dynamic_index_in_dim(rows_of, quarter, axis=0, keepdims=False)
                part = jnp.dot(cols, rows, preferred_element_type=jnp.float32)
                total = part if total is None else total + part
            return total

        projected = None
        for k in (0, 1, 3):
            normed = normalize(pieces[k], k, scale, norm_gain, tp_index)
            part = project(normed, k, tp_index, core_index)
            projected = part if projected is None else projected + part
        projected = lax.optimization_barrier(projected)
        far_piece, far_scale, far_gain, far_tp, far_core = lax.optimization_barrier(
            (pieces[2], scale, norm_gain, tp_index, core_index)
        )
        normed = normalize(far_piece, 2, far_scale, far_gain, far_tp)
        projected = projected + project(normed, 2, far_tp, far_core)
        queries = projected[:, :q_cols]
        key_proj = projected[:, q_cols : q_cols + k_cols]
        value_proj = projected[:, q_cols + k_cols :]
        local_heads = q_cols // HEAD
        local_groups = k_cols // HEAD
        group_size = local_heads // local_groups
        positions = positions_of(segment_ids)
        q_rot = rotate((queries + q_bias).reshape(row_count, local_heads, HEAD), positions).astype(
            jnp.bfloat16
        )
        q_rot = q_rot.reshape(row_count, local_groups, group_size, HEAD)
        k_rot = rotate((key_proj + k_bias).reshape(row_count, local_groups, HEAD), positions).astype(
            jnp.bfloat16
        )
        value_heads = (value_proj + v_bias).astype(jnp.bfloat16).reshape(row_count, local_groups, HEAD)
        block_rows = min(512, row_count)
        row_index = jnp.arange(row_count, dtype=jnp.int32)
        scores = jnp.einsum(
            "qkgd,pkd->kgqp", q_rot, k_rot, preferred_element_type=jnp.float32
        ) / math.sqrt(HEAD)
        allowed = (segment_ids[0:block_rows, None] == segment_ids[None, :block_rows]) & (
            row_index[0:block_rows, None] >= row_index[None, :block_rows]
        )
        scores = jnp.where(allowed[None, None], scores, -jnp.inf)
        highest = jnp.max(scores, axis=-1, keepdims=True)
        expo = jnp.exp(scores - highest)
        probs = (expo / jnp.sum(expo, axis=-1, keepdims=True)).astype(jnp.bfloat16)
        mixed = jnp.einsum("kgqp,pkd->qkgd", probs, value_heads, preferred_element_type=jnp.float32)
        outputs = mixed.astype(jnp.bfloat16).reshape(block_rows, local_heads * HEAD)
        return outputs

    return body


def solution(mesh):
    seq_count, tp_count = mesh.devices.shape
    core_count = 2
    chip_count = seq_count // core_count
    split = Mesh(mesh.devices.reshape(chip_count, core_count, tp_count), (CHIPS, CORE, TP))
    in_specs = (
        P(SEQ, TP),
        P(SEQ),
        P(SEQ),
        P(),
        P(SEQ, TP),
        P(SEQ, TP),
        P(SEQ, TP),
        P(TP),
        P(TP),
        P(TP),
    )
    out_specs = P(SEQ, TP)
    return jax.shard_map(
        make_local(chip_count, core_count, tp_count),
        mesh=split,
        in_specs=in_specs,
        out_specs=out_specs,
        check_vma=False,
    )
```

```python
import math

import jax
import jax.numpy as jnp
from jax import lax
from jax.sharding import Mesh
from jax.sharding import PartitionSpec as P


HEAD = 128


EPS = 1e-06
ROPE_BASE = 1000000.0

CHIPS = "chips"
CORE = "core"
SEQ = (CHIPS, CORE)
TP = "tp"


def rotate(tensor, positions):
    half_size = tensor.shape[-1] // 2
    frequency = jnp.exp(
        jnp.arange(half_size, dtype=jnp.float32) * (-2.0 * math.log(ROPE_BASE) / tensor.shape[-1])
    )
    angles = positions.astype(jnp.float32)[:, None] * frequency[None, :]
    cosine = jnp.cos(angles)[:, None, :]
    sine_part = jnp.sin(angles)[:, None, :]
    front_half = tensor[..., :half_size]
    back_half = tensor[..., half_size:]
    return jnp.concatenate(
        [front_half * cosine - back_half * sine_part, back_half * cosine + front_half * sine_part],
        axis=-1,
    )


def positions_of(segments):
    length = segments.shape[-1]
    counter = jnp.arange(length, dtype=jnp.int32)
    starts = jnp.concatenate([jnp.ones((1,), dtype=bool), segments[1:] != segments[:-1]])
    marked = jnp.where(starts, counter, jnp.zeros_like(counter))
    return counter - lax.cummax(marked, axis=0)


def make_local(chip_count, core_count, tp_count):
    peer_count = chip_count * core_count

    def body(
        rollout_rows, plan, segment_ids, norm_gain, q_weight, k_weight, v_weight, q_bias, k_bias, v_bias
    ):
        row_count, width = rollout_rows.shape
        slots_each = row_count // peer_count + row_count // (4 * peer_count)
        q_cols = q_weight.shape[1]
        k_cols = k_weight.shape[1]


        weights = jnp.concatenate([q_weight, k_weight, v_weight], axis=1)
        own_weights = lax.all_gather(weights, CHIPS, axis=0, tiled=False)
        other_weights = lax.ppermute(
            own_weights, CORE, [(c, (c + 1) % core_count) for c in range(core_count)]
        )

        target = plan // row_count
        learner_slot = plan % row_count
        matches = (target[:, None] == jnp.arange(peer_count, dtype=jnp.int32)[None, :]).astype(
            jnp.int32
        )
        ranking = jnp.sum((jnp.cumsum(matches, axis=0) - 1) * matches, axis=1)
        parcel_rows = -(-(slots_each + 1) // 8) * 8
        flat_slot = target * parcel_rows + ranking
        slot_hits = flat_slot[None, :] == jnp.arange(peer_count * parcel_rows, dtype=jnp.int32)[:, None]
        tagged = jnp.sum(jnp.where(slot_hits, learner_slot[None, :] + 1, 0), axis=1).reshape(
            peer_count, parcel_rows
        )[:, :slots_each]
        tag_row = jnp.concatenate(
            [
                (tagged // 32).astype(jnp.bfloat16),
                (tagged % 32).astype(jnp.bfloat16),
                jnp.zeros((peer_count, width - 2 * slots_each), jnp.bfloat16),
            ],
            axis=1,
        )
        picked = jnp.dot(
            slot_hits.astype(jnp.bfloat16), rollout_rows, preferred_element_type=jnp.float32
        ).astype(jnp.bfloat16).reshape(peer_count, parcel_rows, width)
        row_in_parcel = jnp.arange(parcel_rows, dtype=jnp.int32)[None, :, None]
        payload = jnp.where(row_in_parcel == slots_each, tag_row[:, None, :], picked)
        arrived = lax.all_to_all(payload, SEQ, split_axis=0, concat_axis=0, tiled=True)
        tags = arrived[:, slots_each, : 2 * slots_each].astype(jnp.int32)
        labels = tags[:, :slots_each] * 32 + tags[:, slots_each:] - 1
        labels = jnp.concatenate(
            [labels, jnp.full((peer_count, parcel_rows - slots_each), -1, jnp.int32)], axis=1
        ).reshape(peer_count * parcel_rows)
        row_numbers = jnp.arange(row_count, dtype=jnp.int32)
        label_hits = labels[None, :] == row_numbers[:, None]
        learner_part = jnp.dot(
            label_hits.astype(jnp.bfloat16),
            arrived.reshape(peer_count * parcel_rows, width),
            preferred_element_type=jnp.float32,
        ).astype(jnp.bfloat16)

        tp_index = lax.axis_index(TP)
        core_index = lax.axis_index(CORE)
        wide = learner_part.astype(jnp.float32)
        own_sq = jnp.sum(wide * wide, axis=-1)
        others = [
            lax.ppermute(own_sq, TP, [(t, (t + k) % tp_count) for t in range(tp_count)])
            for k in range(1, tp_count)
        ]
        total_sq = own_sq
        for other in others:
            total_sq = total_sq + other
        scale = lax.rsqrt(total_sq / (width * tp_count) + EPS)[:, None]

        to_right = [(t, (t + 1) % tp_count) for t in range(tp_count)]
        to_left = [(t, (t - 1) % tp_count) for t in range(tp_count)]
        half = width // 2
        from_left = lax.ppermute(learner_part, TP, to_right)
        from_right = lax.ppermute(learner_part, TP, to_left)
        far_a = lax.ppermute(from_left[:, :half], TP, to_right)
        far_b = lax.ppermute(from_right[:, half:], TP, to_left)
        far = jnp.concatenate([far_a, far_b], axis=1)
        pieces = [learner_part, from_left, far, from_right]

        block = width // (4 * core_count)
        span = 4 * block
        own_rows = own_weights.reshape(tp_count, span, own_weights.shape[-1])
        other_rows = other_weights.reshape(tp_count, span, own_weights.shape[-1])

        def core_block(x, c):
            return jnp.concatenate(
                [x[:, (hl * core_count + c) * block : (hl * core_count + c + 1) * block] for hl in range(4)],
                axis=1,
            )

        def normalize(piece, k, scale, norm_gain, tp_index):
            quarter = (tp_index - k) % tp_count
            gain = lax.dynamic_slice_in_dim(norm_gain, quarter * width, width)
            return (piece.astype(jnp.float32) * scale * gain).astype(jnp.bfloat16)

        def project(normed, k, tp_index, core_index):
            quarter = (tp_index - k) % tp_count
            first = core_block(normed, 0)
            second = core_block(normed, 1)
            mine = jnp.where(core_index == 0, first, second)
            theirs = jnp.where(core_index == 0, second, first)
            total = None
            for cols, rows_of in ((mine, own_rows), (theirs, other_rows)):
                rows = lax.dynamic_index_in_dim(rows_of, quarter, axis=0, keepdims=False)
                part = jnp.dot(cols, rows, preferred_element_type=jnp.float32)
                total = part if total is None else total + part
            return total

        projected = None
        for k in (0, 1, 3):
            normed = normalize(pieces[k], k, scale, norm_gain, tp_index)
            part = project(normed, k, tp_index, core_index)
            projected = part if projected is None else projected + part
        projected = lax.optimization_barrier(projected)
        far_quarter = (tp_index - 2) % tp_count
        far_rows = jnp.concatenate(
            [
                lax.dynamic_index_in_dim(own_rows, far_quarter, axis=0, keepdims=False),
                lax.dynamic_index_in_dim(other_rows, far_quarter, axis=0, keepdims=False),
            ],
            axis=0,
        )
        far_piece, far_scale, far_gain, far_tp, far_core = lax.optimization_barrier(
            (pieces[2], scale, norm_gain, tp_index, core_index)
        )
        normed = normalize(far_piece, 2, far_scale, far_gain, far_tp)
        first = core_block(normed, 0)
        second = core_block(normed, 1)
        both = jnp.where(
            far_core == 0,
            jnp.concatenate([first, second], axis=1),
            jnp.concatenate([second, first], axis=1),
        )
        projected = projected + jnp.dot(both, far_rows, preferred_element_type=jnp.float32)
        queries = projected[:, :q_cols]
        key_proj = projected[:, q_cols : q_cols + k_cols]
        value_proj = projected[:, q_cols + k_cols :]
        local_heads = q_cols // HEAD
        local_groups = k_cols // HEAD
        group_size = local_heads // local_groups
        positions = positions_of(segment_ids)
        q_rot = rotate((queries + q_bias).reshape(row_count, local_heads, HEAD), positions).astype(
            jnp.bfloat16
        )
        q_rot = q_rot.reshape(row_count, local_groups, group_size, HEAD)
        k_rot = rotate((key_proj + k_bias).reshape(row_count, local_groups, HEAD), positions).astype(
            jnp.bfloat16
        )
        value_heads = (value_proj + v_bias).astype(jnp.bfloat16).reshape(row_count, local_groups, HEAD)
        block_rows = min(512, row_count)
        row_index = jnp.arange(row_count, dtype=jnp.int32)
        scores = jnp.einsum(
            "qkgd,pkd->kgqp", q_rot, k_rot, preferred_element_type=jnp.float32
        ) / math.sqrt(HEAD)
        allowed = (segment_ids[0:block_rows, None] == segment_ids[None, :block_rows]) & (
            row_index[0:block_rows, None] >= row_index[None, :block_rows]
        )
        scores = jnp.where(allowed[None, None], scores, -jnp.inf)
        highest = jnp.max(scores, axis=-1, keepdims=True)
        expo = jnp.exp(scores - highest)
        probs = (expo / jnp.sum(expo, axis=-1, keepdims=True)).astype(jnp.bfloat16)
        mixed = jnp.einsum("kgqp,pkd->qkgd", probs, value_heads, preferred_element_type=jnp.float32)
        outputs = mixed.astype(jnp.bfloat16).reshape(block_rows, local_heads * HEAD)
        return outputs

    return body


def solution(mesh):
    seq_count, tp_count = mesh.devices.shape
    core_count = 2
    chip_count = seq_count // core_count
    split = Mesh(mesh.devices.reshape(chip_count, core_count, tp_count), (CHIPS, CORE, TP))
    in_specs = (
        P(SEQ, TP),
        P(SEQ),
        P(SEQ),
        P(),
        P(SEQ, TP),
        P(SEQ, TP),
        P(SEQ, TP),
        P(TP),
        P(TP),
        P(TP),
    )
    out_specs = P(SEQ, TP)
    return jax.shard_map(
        make_local(chip_count, core_count, tp_count),
        mesh=split,
        in_specs=in_specs,
        out_specs=out_specs,
        check_vma=False,
    )
```

```python
import math

import jax
import jax.numpy as jnp
from jax import lax
from jax.sharding import Mesh
from jax.sharding import PartitionSpec as P


HEAD = 128


EPS = 1e-06
ROPE_BASE = 1000000.0

CHIPS = "chips"
CORE = "core"
SEQ = (CHIPS, CORE)
TP = "tp"


def rotate(tensor, positions):
    half_size = tensor.shape[-1] // 2
    frequency = jnp.exp(
        jnp.arange(half_size, dtype=jnp.float32) * (-2.0 * math.log(ROPE_BASE) / tensor.shape[-1])
    )
    angles = positions.astype(jnp.float32)[:, None] * frequency[None, :]
    cosine = jnp.cos(angles)[:, None, :]
    sine_part = jnp.sin(angles)[:, None, :]
    front_half = tensor[..., :half_size]
    back_half = tensor[..., half_size:]
    return jnp.concatenate(
        [front_half * cosine - back_half * sine_part, back_half * cosine + front_half * sine_part],
        axis=-1,
    )


def positions_of(segments):
    length = segments.shape[-1]
    counter = jnp.arange(length, dtype=jnp.int32)
    starts = jnp.concatenate([jnp.ones((1,), dtype=bool), segments[1:] != segments[:-1]])
    marked = jnp.where(starts, counter, jnp.zeros_like(counter))
    return counter - lax.cummax(marked, axis=0)


def make_local(chip_count, core_count, tp_count):
    peer_count = chip_count * core_count

    def body(
        rollout_rows, plan, segment_ids, norm_gain, q_weight, k_weight, v_weight, q_bias, k_bias, v_bias
    ):
        row_count, width = rollout_rows.shape
        slots_each = row_count // peer_count + row_count // (4 * peer_count)
        q_cols = q_weight.shape[1]
        k_cols = k_weight.shape[1]


        weights = jnp.concatenate([q_weight, k_weight, v_weight], axis=1)
        own_weights = lax.all_gather(weights, CHIPS, axis=0, tiled=False)
        other_weights = lax.ppermute(
            own_weights, CORE, [(c, (c + 1) % core_count) for c in range(core_count)]
        )

        target = plan // row_count
        learner_slot = plan % row_count
        matches = (target[:, None] == jnp.arange(peer_count, dtype=jnp.int32)[None, :]).astype(
            jnp.int32
        )
        ranking = jnp.sum((jnp.cumsum(matches, axis=0) - 1) * matches, axis=1)
        parcel_rows = -(-(slots_each + 1) // 8) * 8
        flat_slot = target * parcel_rows + ranking
        slot_hits = flat_slot[None, :] == jnp.arange(peer_count * parcel_rows, dtype=jnp.int32)[:, None]
        tagged = jnp.sum(jnp.where(slot_hits, learner_slot[None, :] + 1, 0), axis=1).reshape(
            peer_count, parcel_rows
        )[:, :slots_each]
        tag_row = jnp.concatenate(
            [
                (tagged // 32).astype(jnp.bfloat16),
                (tagged % 32).astype(jnp.bfloat16),
                jnp.zeros((peer_count, width - 2 * slots_each), jnp.bfloat16),
            ],
            axis=1,
        )
        picked = jnp.dot(
            slot_hits.astype(jnp.bfloat16), rollout_rows, preferred_element_type=jnp.float32
        ).astype(jnp.bfloat16).reshape(peer_count, parcel_rows, width)
        row_in_parcel = jnp.arange(parcel_rows, dtype=jnp.int32)[None, :, None]
        payload = jnp.where(row_in_parcel == slots_each, tag_row[:, None, :], picked)
        arrived = lax.all_to_all(payload, SEQ, split_axis=0, concat_axis=0, tiled=True)
        tags = arrived[:, slots_each, : 2 * slots_each].astype(jnp.int32)
        labels = tags[:, :slots_each] * 32 + tags[:, slots_each:] - 1
        labels = jnp.concatenate(
            [labels, jnp.full((peer_count, parcel_rows - slots_each), -1, jnp.int32)], axis=1
        ).reshape(peer_count * parcel_rows)
        row_numbers = jnp.arange(row_count, dtype=jnp.int32)
        label_hits = labels[None, :] == row_numbers[:, None]
        learner_part = jnp.dot(
            label_hits.astype(jnp.bfloat16),
            arrived.reshape(peer_count * parcel_rows, width),
            preferred_element_type=jnp.float32,
        ).astype(jnp.bfloat16)

        tp_index = lax.axis_index(TP)
        core_index = lax.axis_index(CORE)
        wide = learner_part.astype(jnp.float32)
        own_sq = jnp.sum(wide * wide, axis=-1)
        others = [
            lax.ppermute(own_sq, TP, [(t, (t + k) % tp_count) for t in range(tp_count)])
            for k in range(1, tp_count)
        ]
        total_sq = own_sq
        for other in others:
            total_sq = total_sq + other
        scale = lax.rsqrt(total_sq / (width * tp_count) + EPS)[:, None]

        to_right = [(t, (t + 1) % tp_count) for t in range(tp_count)]
        to_left = [(t, (t - 1) % tp_count) for t in range(tp_count)]
        half_rows = row_count // 2
        left_top = lax.ppermute(learner_part[:half_rows], TP, to_right)
        left_bottom = lax.ppermute(learner_part[half_rows:], TP, to_left)
        right_top = lax.ppermute(learner_part[:half_rows], TP, to_left)
        right_bottom = lax.ppermute(learner_part[half_rows:], TP, to_right)
        from_left = jnp.concatenate([left_top, right_bottom], axis=0)
        from_right = jnp.concatenate([right_top, left_bottom], axis=0)
        far_a = lax.ppermute(left_top, TP, to_right)
        far_b = lax.ppermute(left_bottom, TP, to_left)
        far = jnp.concatenate([far_a, far_b], axis=0)
        pieces = [learner_part, from_left, far, from_right]

        block = width // (4 * core_count)
        span = 4 * block
        own_rows = own_weights.reshape(tp_count, span, own_weights.shape[-1])
        other_rows = other_weights.reshape(tp_count, span, own_weights.shape[-1])

        def core_block(x, c):
            return jnp.concatenate(
                [x[:, (hl * core_count + c) * block : (hl * core_count + c + 1) * block] for hl in range(4)],
                axis=1,
            )

        def normalize(piece, k, scale, norm_gain, tp_index):
            quarter = (tp_index - k) % tp_count
            gain = lax.dynamic_slice_in_dim(norm_gain, quarter * width, width)
            return (piece.astype(jnp.float32) * scale * gain).astype(jnp.bfloat16)

        def project(normed, k, tp_index, core_index):
            quarter = (tp_index - k) % tp_count
            first = core_block(normed, 0)
            second = core_block(normed, 1)
            mine = jnp.where(core_index == 0, first, second)
            theirs = jnp.where(core_index == 0, second, first)
            total = None
            for cols, rows_of in ((mine, own_rows), (theirs, other_rows)):
                rows = lax.dynamic_index_in_dim(rows_of, quarter, axis=0, keepdims=False)
                part = jnp.dot(cols, rows, preferred_element_type=jnp.float32)
                total = part if total is None else total + part
            return total

        projected = None
        for k in (0, 1, 3):
            normed = normalize(pieces[k], k, scale, norm_gain, tp_index)
            part = project(normed, k, tp_index, core_index)
            projected = part if projected is None else projected + part
        projected = lax.optimization_barrier(projected)
        far_piece, far_scale, far_gain, far_tp, far_core = lax.optimization_barrier(
            (pieces[2], scale, norm_gain, tp_index, core_index)
        )
        normed = normalize(far_piece, 2, far_scale, far_gain, far_tp)
        projected = projected + project(normed, 2, far_tp, far_core)
        queries = projected[:, :q_cols]
        key_proj = projected[:, q_cols : q_cols + k_cols]
        value_proj = projected[:, q_cols + k_cols :]
        local_heads = q_cols // HEAD
        local_groups = k_cols // HEAD
        group_size = local_heads // local_groups
        positions = positions_of(segment_ids)
        q_rot = rotate((queries + q_bias).reshape(row_count, local_heads, HEAD), positions).astype(
            jnp.bfloat16
        )
        q_rot = q_rot.reshape(row_count, local_groups, group_size, HEAD)
        k_rot = rotate((key_proj + k_bias).reshape(row_count, local_groups, HEAD), positions).astype(
            jnp.bfloat16
        )
        value_heads = (value_proj + v_bias).astype(jnp.bfloat16).reshape(row_count, local_groups, HEAD)
        block_rows = min(512, row_count)
        row_index = jnp.arange(row_count, dtype=jnp.int32)
        scores = jnp.einsum(
            "qkgd,pkd->kgqp", q_rot, k_rot, preferred_element_type=jnp.float32
        ) / math.sqrt(HEAD)
        allowed = (segment_ids[0:block_rows, None] == segment_ids[None, :block_rows]) & (
            row_index[0:block_rows, None] >= row_index[None, :block_rows]
        )
        scores = jnp.where(allowed[None, None], scores, -jnp.inf)
        highest = jnp.max(scores, axis=-1, keepdims=True)
        expo = jnp.exp(scores - highest)
        probs = (expo / jnp.sum(expo, axis=-1, keepdims=True)).astype(jnp.bfloat16)
        mixed = jnp.einsum("kgqp,pkd->qkgd", probs, value_heads, preferred_element_type=jnp.float32)
        outputs = mixed.astype(jnp.bfloat16).reshape(block_rows, local_heads * HEAD)
        return outputs

    return body


def solution(mesh):
    seq_count, tp_count = mesh.devices.shape
    core_count = 2
    chip_count = seq_count // core_count
    split = Mesh(mesh.devices.reshape(chip_count, core_count, tp_count), (CHIPS, CORE, TP))
    in_specs = (
        P(SEQ, TP),
        P(SEQ),
        P(SEQ),
        P(),
        P(SEQ, TP),
        P(SEQ, TP),
        P(SEQ, TP),
        P(TP),
        P(TP),
        P(TP),
    )
    out_specs = P(SEQ, TP)
    return jax.shard_map(
        make_local(chip_count, core_count, tp_count),
        mesh=split,
        in_specs=in_specs,
        out_specs=out_specs,
        check_vma=False,
    )
```
